256 devices in a mesh: grp: 8 (over z), dev: 32 (over x, y, core).
Axes of the slice: x: 4, y: 4, z: 8, core: 2. Of those that a mesh axis runs over, the one named last changes fastest.
Arguments:
- particles: bfloat16 [8192, 16384], P(('grp', 'dev')), may hold values from -60 to 60
- particle_precision: bfloat16 [8192], P(('grp', 'dev')), may hold values from 0.5 to 4
- particle_class: int32 [8192, 1], P(('grp', 'dev')), may hold values from 0 to 31; in each aligned block of 32 rows (0 to 31, 32 to 63, ...) at most 2 rows name the same one
- class_owner: int32 [32], replicated, may hold values from 0 to 31, each once
- references: bfloat16 [32, 48, 16384], P('dev'), may hold values from -0.08984375 to 0.08984375
- insert_weights: float32 [256, 48], P('dev'), may hold values from -0.875 to 0.875
Outputs:
- volume: float32 [256, 256, 256], P('grp', 'dev')
- evidence: float32 [8192], P(('grp', 'dev'))
The draws below stay inside these ranges and needn't reach their ends.
Inputs may be any that keep to these rules, and one draw needn't show every extreme that they name: `particle_class`: within the 32 particles of one device no class appears more than 2 times, and some class does exactly 2 times.
All inputs are finite; a program needn't handle non-finite values.
Results may differ from the reference program's by a relative error of at most 0.0026.
Values may be sent and summed in bfloat16 or wider, within the bound.
No kernel may reach another device: no remote copies, remote signals or barrier semaphores. Data moves between devices by JAX's collectives and lax.ppermute only.
A program may use at most 128 MiB of HBM per device.

```python
import math
import jax
import jax.numpy as jnp
import numpy as np
from jax import lax

IMG = 128
PIX = 16384
VOL = 256
K = 48
CLS_DEV = 1
P_DEV = 32
CLASSES = 32
SLOT = 2
ZD = 8
PARTICLES = 8192
N_GRP = 8
N_DEV = 32


def draw_particles(key, part):
    first_key = jax.random.fold_in(key, 0)
    values = jnp.clip(jax.random.normal(first_key, (PARTICLES, PIX), jnp.float32), -6.0, 6.0)
    return values.astype(jnp.bfloat16)


def level_of(stream_key, shape, cuts, smallest, largest):
    factor_of = 1.0
    for dim, shards_of in cuts:
        draws = jax.random.uniform(jax.random.fold_in(jax.random.fold_in(stream_key, 6), dim), (shards_of,), jnp.float32, smallest / len(cuts), largest / len(cuts))
        factor_of = factor_of * jnp.repeat(jnp.exp(draws), shape[dim] // shards_of).reshape((-1,) + (1,) * (len(shape) - 1 - dim))
    return factor_of


def assign_block(own_key, own, number, rows, count, top, most, lean):
    sequence = jax.random.permutation(own_key, count)
    heavy_load, ordinary = load_shares(count, rows * top, most, lean, True), load_shares(count, rows * top, most, lean, False)
    places = jnp.arange(count)

    def named(lengths, rotation):
        used = int((lengths > 0).sum())
        fixed = max(1, used // 4)
        moved = fixed + (places - fixed + rotation * (used - fixed)) % max(1, count - fixed)
        return jnp.zeros((count,), jnp.int32).at[sequence[jnp.where(places < fixed, places, moved)]].set(jnp.asarray(lengths, jnp.int32))

    lengths = jnp.where(number % 4 == 0, named(heavy_load, number // 4), named(ordinary, number - number // 4 - 1))
    mixed = jax.random.permutation(jax.random.fold_in(own, 3), count)
    giver, sink = mixed[0:count // 2 * 2:2], mixed[1:count // 2 * 2:2]
    slack = jnp.minimum(lengths[giver] - 1, most - lengths[sink]) // 2
    slack = jnp.where((giver == sequence[0]) | (sink == sequence[0]) | (lengths[sink] == 0), 0, jnp.maximum(slack, 0))
    moved = jax.random.randint(jax.random.fold_in(own, 4), (count // 2,), 0, 1 << 20) % (slack + 1)
    lengths = lengths.at[giver].add(-moved).at[sink].add(moved)
    items = jnp.searchsorted(jnp.cumsum(lengths), jnp.arange(rows * top), side="right").astype(jnp.int32)
    listing = items.reshape(top, rows).T
    listing = listing[jax.random.permutation(jax.random.fold_in(own, 1), rows)]
    rotation = jax.random.randint(jax.random.fold_in(own, 2), (rows, 1), 0, top)
    return jnp.take_along_axis(listing, (jnp.arange(top)[None, :] + rotation) % top, axis=1)


def load_shares(amount, total, reach, lean, full):
    weights = [(1 << 20) // math.isqrt(grade ** lean) + 1 for grade in range(1, amount + 1)]
    largest = reach if full else min(reach, max(-(-total // amount), total * weights[0] // sum(weights)))
    least = 1 if total - largest >= amount - 1 else 0
    counts, rest = [largest] + [least] * (amount - 1), total - largest - least * (amount - 1)
    while rest > 0:
        candidates = [i for i in range(1, amount) if counts[i] < largest] or [i for i in range(1, amount) if counts[i] < reach]
        pool, budget = sum([weights[i] for i in candidates]), rest
        for i in candidates:
            extra = min(reach - counts[i], max(1, budget * weights[i] // pool), rest)
            counts[i] = counts[i] + extra
            rest = rest - extra
    return np.array(counts)


def noise(stream_key, dims, scale, bound, shards=(), held_as=jnp.bfloat16):
    gain = level_of(stream_key, dims, shards, -0.22, 0.18) if shards else 1.0
    drawn = jax.random.normal(stream_key, dims, jnp.float32) * scale * gain
    return jnp.minimum(jnp.maximum(drawn, -bound), bound).astype(held_as)


def setup_inputs(seed: int = 0) -> dict:
    seeds = jax.random.split(jax.random.key(seed), 7)
    particles = draw_particles(jax.random.fold_in(seeds[6], 71), 0)
    particle_precision = jnp.clip(jnp.exp(math.log(4.0) - 2.0794415 * jax.random.uniform(seeds[1], (PARTICLES,), jnp.float32) ** level_of(seeds[1], (PARTICLES,), ((0, 256),), -0.2, 0.2)), 0.5, 4.0).astype(jnp.bfloat16)
    particle_class_keys = jax.random.split(jax.random.fold_in(seeds[2], 1), PARTICLES // P_DEV)
    particle_class_turns = jax.random.permutation(jax.random.fold_in(seeds[2], 3), PARTICLES // P_DEV)
    particle_class = jax.vmap(lambda own, number: assign_block(jax.random.fold_in(seeds[2], 2), own, number, P_DEV, CLASSES, 1, SLOT, 2))(particle_class_keys, particle_class_turns).reshape((PARTICLES, 1))
    class_owner = jax.random.permutation(seeds[3], CLASSES).astype(jnp.int32)
    references = noise(seeds[4], (CLASSES, K, PIX), 0.015625, 0.08984375, ((0, 32),))
    insert_weights = noise(seeds[5], (VOL, CLS_DEV * K), (CLS_DEV * K) ** -0.5, 0.875, ((0, 32),), jnp.float32)
    return {"particles": particles, "particle_precision": particle_precision, "particle_class": particle_class, "class_owner": class_owner, "references": references, "insert_weights": insert_weights}


OFFSETS = [(-1, -1), (-1, 0), (-1, 1), (0, -1), (0, 0), (0, 1), (1, -1), (1, 0), (1, 1)]


def upsample_table(length, source):
    target = jnp.arange(length, dtype=jnp.int32)[:, None]
    anchor = jnp.arange(source, dtype=jnp.int32)[None, :]
    halves = target // 2
    lower = anchor == halves
    upper = anchor == (halves + 1) % source
    is_even = (target % 2) == 0
    even_part = jnp.where(lower, 1.0, 0.0)
    odd_part = jnp.where(lower, 0.5, 0.0) + jnp.where(upper, 0.5, 0.0)
    return jnp.where(is_even, even_part, odd_part).astype(jnp.float32)


def class_pass(row_data, scales, templates):
    refcount = templates.shape[0]
    picture = templates.reshape(refcount, IMG, IMG)
    rotated = jnp.concatenate([jnp.roll(picture, (-offset[0], -offset[1]), (1, 2)).reshape(refcount, IMG * IMG) for offset in OFFSETS], 0)
    energy = jnp.sum(jnp.square(templates.astype(jnp.float32)), axis=1)
    energy = jnp.tile(energy, len(OFFSETS))
    products = lax.dot_general(rotated, row_data, (((1,), (1,)), ((), ())), preferred_element_type=jnp.float32)
    scores = scales.astype(jnp.float32)[None, :] * (products - 0.5 * energy[:, None])
    highest = jnp.max(scores, axis=0)
    evidence = highest + jnp.log(jnp.sum(jnp.exp(scores - highest[None, :]), axis=0))
    weights = jnp.exp(scores - evidence[None, :]).astype(jnp.bfloat16)
    partials = jnp.dot(weights, row_data, preferred_element_type=jnp.float32).reshape(len(OFFSETS), refcount, IMG, IMG)
    summed = jnp.zeros((refcount, IMG, IMG), jnp.float32)
    for number, offset in enumerate(OFFSETS):
        summed = summed + jnp.roll(partials[number], offset, (1, 2))
    return summed.reshape(refcount, IMG * IMG), evidence


def reference(particles, particle_precision, particle_class, class_owner, references, insert_weights):
    pictures = particles.reshape(N_GRP, N_DEV, P_DEV, PIX)
    precisions = particle_precision.reshape(N_GRP, N_DEV, P_DEV)
    labels_all = particle_class.reshape(N_GRP, N_DEV, P_DEV)
    interp = upsample_table(VOL, IMG)
    ordinal = jnp.arange(P_DEV, dtype=jnp.int32)
    sources = jnp.broadcast_to(jnp.arange(N_DEV, dtype=jnp.int32)[:, None], (N_DEV, P_DEV))

    def group_pass(inputs):
        group_pictures, group_scales, group_labels = inputs
        position = class_owner[group_labels].astype(jnp.int32)
        earlier = (group_labels[:, :, None] == group_labels[:, None, :]) & (ordinal[None, :] < ordinal[:, None])[None]
        arrival = jnp.sum(earlier, axis=2).astype(jnp.int32)
        slot_index = position * SLOT + arrival
        buffer = jnp.zeros((N_DEV, CLASSES * SLOT, PIX), jnp.bfloat16).at[sources, slot_index].set(group_pictures)
        scale_buffer = jnp.zeros((N_DEV, CLASSES * SLOT), jnp.bfloat16).at[sources, slot_index].set(group_scales)
        buffer = buffer.reshape(N_DEV, CLASSES, SLOT, PIX).transpose(1, 0, 2, 3).reshape(CLASSES, N_DEV * SLOT, PIX)
        scale_buffer = scale_buffer.reshape(N_DEV, CLASSES, SLOT).transpose(1, 0, 2).reshape(CLASSES, N_DEV * SLOT)
        class_sums, class_evidence = lax.map(lambda entry: class_pass(entry[0], entry[1], entry[2]), (buffer, scale_buffer, references))
        class_evidence = class_evidence.reshape(CLASSES, N_DEV, SLOT)
        particle_evidence = class_evidence[position, sources, arrival]
        class_sums = class_sums.reshape(N_DEV, CLS_DEV * K, PIX)
        gains = insert_weights.reshape(N_DEV, ZD, CLS_DEV * K)
        planes = jnp.einsum("dzj,djp->dzp", gains, class_sums, precision=lax.Precision.HIGHEST).reshape(VOL, PIX)
        return planes, particle_evidence

    planes, evidence = lax.map(group_pass, (pictures, precisions, labels_all))
    total = jnp.sum(planes, axis=0).reshape(VOL, IMG, IMG)
    across = jnp.einsum("zuv,xv->zux", total, interp, precision=lax.Precision.HIGHEST)
    volume = jnp.einsum("yu,zux->yzx", interp, across, precision=lax.Precision.HIGHEST)
    return volume, evidence.reshape(PARTICLES)
```

```python
import functools

import jax
import jax.numpy as jnp
from jax import lax
from jax.experimental import pallas as pl
from jax.experimental.pallas import tpu as pltpu
from jax.sharding import PartitionSpec as P

IMG = 128
VOL = 256
SHIFTS = (-1, 0, 1)
TK = 2048
TN = 1024


def upsample_table(length, source):
    target = jnp.arange(length, dtype=jnp.int32)[:, None]
    anchor = jnp.arange(source, dtype=jnp.int32)[None, :]
    halves = target // 2
    lower = anchor == halves
    upper = anchor == (halves + 1) % source
    is_even = target % 2 == 0
    even_part = jnp.where(lower, 1.0, 0.0)
    odd_part = jnp.where(lower, 0.5, 0.0) + jnp.where(upper, 0.5, 0.0)
    return jnp.where(is_even, even_part, odd_part).astype(jnp.float32)


def local_table(rows, anchors):
    target = jnp.arange(rows, dtype=jnp.int32)[:, None]
    anchor = jnp.arange(anchors, dtype=jnp.int32)[None, :]
    halves = target // 2
    lower = anchor == halves
    upper = anchor == halves + 1
    is_even = target % 2 == 0
    even_part = jnp.where(lower, 1.0, 0.0)
    odd_part = jnp.where(lower, 0.5, 0.0) + jnp.where(upper, 0.5, 0.0)
    return jnp.where(is_even, even_part, odd_part).astype(jnp.float32)


def class_kernel(pix, rows_ref, ref_ref, scale_ref, energy_ref, sums_ref, evid_ref,
                 ext_ref, acc_ref, w_ref):
    chunks = pix // IMG

    def build(u, carry):
        off = pl.multiple_of(u * IMG, IMG)
        dst = pl.multiple_of(off + IMG, IMG)
        chunk = rows_ref[:, pl.ds(off, IMG)]
        wide = chunk.astype(jnp.float32)
        ext_ref[0, :, pl.ds(dst, IMG)] = pltpu.roll(wide, IMG - 1, 1).astype(jnp.bfloat16)
        ext_ref[1, :, pl.ds(dst, IMG)] = chunk
        ext_ref[2, :, pl.ds(dst, IMG)] = pltpu.roll(wide, 1, 1).astype(jnp.bfloat16)
        return carry

    lax.fori_loop(0, chunks, build, 0, unroll=8)
    ext_ref[:, :, 0:IMG] = ext_ref[:, :, pix:pix + IMG]
    ext_ref[:, :, pix + IMG:pix + 2 * IMG] = ext_ref[:, :, IMG:2 * IMG]

    acc_ref[...] = jnp.zeros_like(acc_ref)

    def products(j, carry):
        k0 = pl.multiple_of(j * TK, TK)
        tile = ref_ref[:, pl.ds(k0, TK)]
        for ai, a in enumerate(SHIFTS):
            start = pl.multiple_of(k0 + IMG * (1 - a), IMG)
            for bi in range(3):
                moved = ext_ref[bi, :, pl.ds(start, TK)]
                acc_ref[ai * 3 + bi] += lax.dot_general(
                    tile, moved, (((1,), (1,)), ((), ())), preferred_element_type=jnp.float32
                )
        return carry

    lax.fori_loop(0, pix // TK, products, 0)

    scale = scale_ref[...]
    half_energy = 0.5 * energy_ref[...]
    scores = [scale * (acc_ref[t] - half_energy) for t in range(9)]
    highest = jnp.max(scores[0], axis=0, keepdims=True)
    for t in range(1, 9):
        highest = jnp.maximum(highest, jnp.max(scores[t], axis=0, keepdims=True))
    total = jnp.sum(jnp.exp(scores[0] - highest), axis=0, keepdims=True)
    for t in range(1, 9):
        total = total + jnp.sum(jnp.exp(scores[t] - highest), axis=0, keepdims=True)
    evidence = highest + jnp.log(total)
    evid_ref[...] = evidence
    for t in range(9):
        w_ref[t] = jnp.exp(scores[t] - evidence).astype(jnp.bfloat16)

    def class_sums(j, carry):
        n0 = pl.multiple_of(j * TN, TN)
        summed = jnp.zeros(sums_ref[:, pl.ds(0, TN)].shape, jnp.float32)
        for ai, a in enumerate(SHIFTS):
            start = pl.multiple_of(n0 + IMG * (1 - a), IMG)
            for bi in range(3):
                summed = summed + jnp.dot(
                    w_ref[ai * 3 + bi], ext_ref[bi, :, pl.ds(start, TN)],
                    preferred_element_type=jnp.float32,
                )
        sums_ref[:, pl.ds(n0, TN)] = summed
        return carry

    lax.fori_loop(0, pix // TN, class_sums, 0)


def class_pass(rows_ext, templates, scale_row, energy_col, pix):
    rowcount = rows_ext.shape[0]
    refcount = templates.shape[0]
    vmem = pl.BlockSpec(memory_space=pltpu.VMEM)
    flops = 2 * 2 * 9 * refcount * rowcount * pix
    cost = pl.CostEstimate(
        flops=flops, transcendentals=10 * refcount * rowcount,
        bytes_accessed=rows_ext.size * 2 + templates.size * 2 + refcount * pix * 4,
    )
    return pl.pallas_call(
        functools.partial(class_kernel, pix),
        out_shape=(
            jax.ShapeDtypeStruct((refcount, pix), jnp.float32),
            jax.ShapeDtypeStruct((1, rowcount), jnp.float32),
        ),
        in_specs=[vmem] * 4,
        out_specs=(vmem, vmem),
        scratch_shapes=[
            pltpu.VMEM((3, rowcount, pix + 2 * IMG), jnp.bfloat16),
            pltpu.VMEM((9, refcount, rowcount), jnp.float32),
            pltpu.VMEM((9, refcount, rowcount), jnp.bfloat16),
        ],
        compiler_params=pltpu.CompilerParams(vmem_limit_bytes=48 * 1024 * 1024),
        cost_estimate=cost,
    )(rows_ext, templates, scale_row, energy_col)


def on_device(
    particles, particle_precision, particle_class, class_owner, references, insert_weights
):
    sources = lax.axis_size("dev")
    groups = lax.axis_size("grp")
    local_count, pix = particles.shape
    classes = class_owner.shape[0]
    owned_classes = references.shape[0]
    slot_depth = max(2, 2 * local_count // classes)
    labels = particle_class[:, 0]
    catalog = jnp.arange(classes, dtype=jnp.int32)
    position = jnp.sum(
        jnp.where(labels[:, None] == catalog[None, :], class_owner[None, :], 0), axis=1
    )
    ordinal = jnp.arange(local_count, dtype=jnp.int32)
    earlier = (labels[:, None] == labels[None, :]) & (ordinal[None, :] < ordinal[:, None])
    arrival = jnp.sum(earlier, axis=1)
    slot_index = position * slot_depth + arrival
    total_slots = classes * slot_depth
    placing = (jnp.arange(total_slots, dtype=jnp.int32)[:, None] == slot_index[None, :]).astype(
        jnp.bfloat16
    )
    extra = jnp.broadcast_to(particle_precision[:, None], (local_count, IMG))
    carried = jnp.concatenate([particles, extra], axis=1)
    width = pix + IMG
    outgoing = jnp.dot(placing, carried, preferred_element_type=jnp.float32).astype(jnp.bfloat16)
    outgoing = outgoing.reshape(sources, owned_classes * slot_depth, width)
    arrived = lax.all_to_all(outgoing, "dev", split_axis=0, concat_axis=0, tiled=True)
    rows_ext = arrived.reshape(sources * slot_depth, width)
    scale_row = rows_ext[:, pix].astype(jnp.float32).reshape(1, sources * slot_depth)
    templates = references[0]
    energy_col = jnp.sum(jnp.square(templates.astype(jnp.float32)), axis=1).reshape(-1, 1)
    summed, class_evidence = class_pass(rows_ext, templates, scale_row, energy_col, pix)
    stacked = class_evidence.reshape(sources, owned_classes * slot_depth)
    returned = lax.all_to_all(stacked, "dev", split_axis=0, concat_axis=0, tiled=True).reshape(
        total_slots
    )
    particle_evidence = jnp.take(returned, slot_index)
    planes = jnp.dot(
        insert_weights, summed, precision=lax.Precision.HIGHEST, preferred_element_type=jnp.float32
    )
    depth = planes.shape[0]
    planes = planes.reshape(depth, IMG, IMG)
    band = IMG // groups
    wrapped = jnp.concatenate([planes, planes[:, :1]], axis=1)
    windows = jnp.stack([wrapped[:, g * band:g * band + band + 1] for g in range(groups)], 0)
    mine = lax.psum_scatter(windows, "grp", scatter_dimension=0, tiled=True)[0]
    interp = upsample_table(VOL, IMG)
    across = jnp.einsum("zjv,xv->zjx", mine, interp, precision=lax.Precision.HIGHEST)
    rows_table = local_table(2 * band, band + 1)
    volume = jnp.einsum("yj,zjx->yzx", rows_table, across, precision=lax.Precision.HIGHEST)
    return (volume, particle_evidence)


def solution(mesh):
    placed = (
        P(("grp", "dev"), None),
        P(("grp", "dev")),
        P(("grp", "dev"), None),
        P(),
        P("dev", None, None),
        P("dev", None),
    )
    return jax.shard_map(
        on_device,
        mesh=mesh,
        in_specs=placed,
        out_specs=(P("grp", "dev", None), P(("grp", "dev"))),
        check_vma=False,
    )
```

```python
import functools

import jax
import jax.numpy as jnp
from jax import lax
from jax.experimental import pallas as pl
from jax.experimental.pallas import tpu as pltpu
from jax.sharding import PartitionSpec as P

IMG = 128
VOL = 256
SHIFTS = (-1, 0, 1)
TK = 2048
TN = 1024


def upsample_table(length, source):
    target = jnp.arange(length, dtype=jnp.int32)[:, None]
    anchor = jnp.arange(source, dtype=jnp.int32)[None, :]
    halves = target // 2
    lower = anchor == halves
    upper = anchor == (halves + 1) % source
    is_even = target % 2 == 0
    even_part = jnp.where(lower, 1.0, 0.0)
    odd_part = jnp.where(lower, 0.5, 0.0) + jnp.where(upper, 0.5, 0.0)
    return jnp.where(is_even, even_part, odd_part).astype(jnp.float32)


def local_table(rows, anchors):
    target = jnp.arange(rows, dtype=jnp.int32)[:, None]
    anchor = jnp.arange(anchors, dtype=jnp.int32)[None, :]
    halves = target // 2
    lower = anchor == halves
    upper = anchor == halves + 1
    is_even = target % 2 == 0
    even_part = jnp.where(lower, 1.0, 0.0)
    odd_part = jnp.where(lower, 0.5, 0.0) + jnp.where(upper, 0.5, 0.0)
    return jnp.where(is_even, even_part, odd_part).astype(jnp.float32)


def class_kernel(pix, rows_ref, ref_ref, scale_ref, energy_ref, gain_ref, planes_ref, evid_ref,
                 ext_ref, acc_ref, v_ref):
    chunks = pix // IMG

    def build(u, carry):
        off = pl.multiple_of(u * IMG, IMG)
        dst = pl.multiple_of(off + IMG, IMG)
        chunk = rows_ref[:, pl.ds(off, IMG)]
        wide = chunk.astype(jnp.float32)
        ext_ref[0, :, pl.ds(dst, IMG)] = pltpu.roll(wide, IMG - 1, 1).astype(jnp.bfloat16)
        ext_ref[1, :, pl.ds(dst, IMG)] = chunk
        ext_ref[2, :, pl.ds(dst, IMG)] = pltpu.roll(wide, 1, 1).astype(jnp.bfloat16)
        return carry

    lax.fori_loop(0, chunks, build, 0, unroll=8)
    ext_ref[:, :, 0:IMG] = ext_ref[:, :, pix:pix + IMG]
    ext_ref[:, :, pix + IMG:pix + 2 * IMG] = ext_ref[:, :, IMG:2 * IMG]

    acc_ref[...] = jnp.zeros_like(acc_ref)

    def products(j, carry):
        k0 = pl.multiple_of(j * TK, TK)
        tile = ref_ref[:, pl.ds(k0, TK)]
        for ai, a in enumerate(SHIFTS):
            start = pl.multiple_of(k0 + IMG * (1 - a), IMG)
            for bi in range(3):
                moved = ext_ref[bi, :, pl.ds(start, TK)]
                acc_ref[ai * 3 + bi] += lax.dot_general(
                    tile, moved, (((1,), (1,)), ((), ())), preferred_element_type=jnp.float32
                )
        return carry

    lax.fori_loop(0, pix // TK, products, 0)

    scale = scale_ref[...]
    half_energy = 0.5 * energy_ref[...]
    scores = [scale * (acc_ref[t] - half_energy) for t in range(9)]
    highest = jnp.max(scores[0], axis=0, keepdims=True)
    for t in range(1, 9):
        highest = jnp.maximum(highest, jnp.max(scores[t], axis=0, keepdims=True))
    total = jnp.sum(jnp.exp(scores[0] - highest), axis=0, keepdims=True)
    for t in range(1, 9):
        total = total + jnp.sum(jnp.exp(scores[t] - highest), axis=0, keepdims=True)
    evidence = highest + jnp.log(total)
    evid_ref[...] = evidence
    gain = gain_ref[...]
    gain_hi = gain.astype(jnp.bfloat16)
    gain_lo = (gain - gain_hi.astype(jnp.float32)).astype(jnp.bfloat16)
    depth = gain.shape[0]
    for t in range(9):
        weights = jnp.exp(scores[t] - evidence).astype(jnp.bfloat16)
        mixed = jnp.dot(gain_hi, weights, preferred_element_type=jnp.float32) + jnp.dot(
            gain_lo, weights, preferred_element_type=jnp.float32
        )
        mixed_hi = mixed.astype(jnp.bfloat16).astype(jnp.float32)
        v_ref[t, 0:depth] = mixed_hi
        v_ref[t, depth:2 * depth] = mixed - mixed_hi

    def plane_tiles(j, carry):
        n0 = pl.multiple_of(j * TN, TN)
        summed = jnp.zeros((2 * depth, TN), jnp.float32)
        for ai, a in enumerate(SHIFTS):
            start = pl.multiple_of(n0 + IMG * (1 - a), IMG)
            for bi in range(3):
                summed = summed + jnp.dot(
                    v_ref[ai * 3 + bi].astype(jnp.bfloat16), ext_ref[bi, :, pl.ds(start, TN)],
                    preferred_element_type=jnp.float32,
                )
        planes_ref[:, pl.ds(n0, TN)] = summed[0:depth] + summed[depth:2 * depth]
        return carry

    lax.fori_loop(0, pix // TN, plane_tiles, 0)


def class_pass(rows_ext, templates, scale_row, energy_col, gain, pix):
    rowcount = rows_ext.shape[0]
    refcount = templates.shape[0]
    depth = gain.shape[0]
    vmem = pl.BlockSpec(memory_space=pltpu.VMEM)
    flops = 2 * 9 * (refcount + 2 * depth) * rowcount * pix
    cost = pl.CostEstimate(
        flops=flops, transcendentals=10 * refcount * rowcount,
        bytes_accessed=rows_ext.size * 2 + templates.size * 2 + depth * pix * 4,
    )
    return pl.pallas_call(
        functools.partial(class_kernel, pix),
        out_shape=(
            jax.ShapeDtypeStruct((depth, pix), jnp.float32),
            jax.ShapeDtypeStruct((1, rowcount), jnp.float32),
        ),
        in_specs=[vmem] * 5,
        out_specs=(vmem, vmem),
        scratch_shapes=[
            pltpu.VMEM((3, rowcount, pix + 2 * IMG), jnp.bfloat16),
            pltpu.VMEM((9, refcount, rowcount), jnp.float32),
            pltpu.VMEM((9, 2 * depth, rowcount), jnp.float32),
        ],
        compiler_params=pltpu.CompilerParams(vmem_limit_bytes=48 * 1024 * 1024),
        cost_estimate=cost,
    )(rows_ext, templates, scale_row, energy_col, gain)


def on_device(
    particles, particle_precision, particle_class, class_owner, references, insert_weights
):
    sources = lax.axis_size("dev")
    groups = lax.axis_size("grp")
    local_count, pix = particles.shape
    classes = class_owner.shape[0]
    owned_classes = references.shape[0]
    slot_depth = max(2, 2 * local_count // classes)
    labels = particle_class[:, 0]
    catalog = jnp.arange(classes, dtype=jnp.int32)
    position = jnp.sum(
        jnp.where(labels[:, None] == catalog[None, :], class_owner[None, :], 0), axis=1
    )
    ordinal = jnp.arange(local_count, dtype=jnp.int32)
    earlier = (labels[:, None] == labels[None, :]) & (ordinal[None, :] < ordinal[:, None])
    arrival = jnp.sum(earlier, axis=1)
    slot_index = arrival * classes + position
    total_slots = classes * slot_depth
    placing = (jnp.arange(total_slots, dtype=jnp.int32)[:, None] == slot_index[None, :]).astype(
        jnp.bfloat16
    )
    extra = jnp.broadcast_to(particle_precision[:, None], (local_count, IMG))
    carried = jnp.concatenate([particles, extra], axis=1)
    width = pix + IMG
    outgoing = jnp.dot(placing, carried, preferred_element_type=jnp.float32).astype(jnp.bfloat16)
    outgoing = outgoing.reshape(slot_depth, sources, owned_classes * width)
    arrived = lax.all_to_all(outgoing, "dev", split_axis=1, concat_axis=1, tiled=True)
    rows_ext = arrived.reshape(slot_depth * sources, width)
    scale_row = rows_ext[:, pix].astype(jnp.float32).reshape(1, slot_depth * sources)
    templates = references[0]
    energy_col = jnp.sum(jnp.square(templates.astype(jnp.float32)), axis=1).reshape(-1, 1)
    planes, class_evidence = class_pass(
        rows_ext, templates, scale_row, energy_col, insert_weights, pix
    )
    stacked = class_evidence.reshape(slot_depth, sources)
    returned = lax.all_to_all(stacked, "dev", split_axis=1, concat_axis=1, tiled=True).reshape(
        total_slots
    )
    particle_evidence = jnp.take(returned, slot_index)
    depth = planes.shape[0]
    planes = planes.reshape(depth, IMG, IMG)
    band = IMG // groups
    wrapped = jnp.concatenate([planes, planes[:, :1]], axis=1)
    windows = jnp.stack([wrapped[:, g * band:g * band + band + 1] for g in range(groups)], 0)
    mine = jnp.sum(lax.all_to_all(windows, "grp", split_axis=0, concat_axis=0, tiled=True), 0)
    interp = upsample_table(VOL, IMG)
    across = jnp.einsum("zjv,xv->zjx", mine, interp, precision=lax.Precision.HIGHEST)
    rows_table = local_table(2 * band, band + 1)
    volume = jnp.einsum("yj,zjx->yzx", rows_table, across, precision=lax.Precision.HIGHEST)
    return (volume, particle_evidence)


def solution(mesh):
    placed = (
        P(("grp", "dev"), None),
        P(("grp", "dev")),
        P(("grp", "dev"), None),
        P(),
        P("dev", None, None),
        P("dev", None),
    )
    return jax.shard_map(
        on_device,
        mesh=mesh,
        in_specs=placed,
        out_specs=(P("grp", "dev", None), P(("grp", "dev"))),
        check_vma=False,
    )
```

```python
import functools

import jax
import jax.numpy as jnp
from jax import lax
from jax.experimental import pallas as pl
from jax.experimental.pallas import tpu as pltpu
from jax.sharding import PartitionSpec as P

IMG = 128
VOL = 256
SHIFTS = (-1, 0, 1)
TK = 2048
TN = 1024


def upsample_table(length, source):
    target = jnp.arange(length, dtype=jnp.int32)[:, None]
    anchor = jnp.arange(source, dtype=jnp.int32)[None, :]
    halves = target // 2
    lower = anchor == halves
    upper = anchor == (halves + 1) % source
    is_even = target % 2 == 0
    even_part = jnp.where(lower, 1.0, 0.0)
    odd_part = jnp.where(lower, 0.5, 0.0) + jnp.where(upper, 0.5, 0.0)
    return jnp.where(is_even, even_part, odd_part).astype(jnp.float32)


def local_table(rows, anchors):
    target = jnp.arange(rows, dtype=jnp.int32)[:, None]
    anchor = jnp.arange(anchors, dtype=jnp.int32)[None, :]
    halves = target // 2
    lower = anchor == halves
    upper = anchor == halves + 1
    is_even = target % 2 == 0
    even_part = jnp.where(lower, 1.0, 0.0)
    odd_part = jnp.where(lower, 0.5, 0.0) + jnp.where(upper, 0.5, 0.0)
    return jnp.where(is_even, even_part, odd_part).astype(jnp.float32)


def class_kernel(pix, groups, rows_ref, ref_ref, scale_ref, energy_ref, gain_ref, planes_ref, evid_ref,
                 ext_ref, acc_ref, v_ref):
    chunks = pix // IMG

    def build(u, carry):
        off = pl.multiple_of(u * IMG, IMG)
        dst = pl.multiple_of(off + IMG, IMG)
        chunk = rows_ref[:, pl.ds(off, IMG)]
        wide = chunk.astype(jnp.float32)
        ext_ref[0, :, pl.ds(dst, IMG)] = pltpu.roll(wide, IMG - 1, 1).astype(jnp.bfloat16)
        ext_ref[1, :, pl.ds(dst, IMG)] = chunk
        ext_ref[2, :, pl.ds(dst, IMG)] = pltpu.roll(wide, 1, 1).astype(jnp.bfloat16)
        return carry

    lax.fori_loop(0, chunks, build, 0, unroll=8)
    ext_ref[:, :, 0:IMG] = ext_ref[:, :, pix:pix + IMG]
    ext_ref[:, :, pix + IMG:pix + 2 * IMG] = ext_ref[:, :, IMG:2 * IMG]

    acc_ref[...] = jnp.zeros_like(acc_ref)

    def products(j, carry):
        k0 = pl.multiple_of(j * TK, TK)
        tile = ref_ref[:, pl.ds(k0, TK)]
        for ai, a in enumerate(SHIFTS):
            start = pl.multiple_of(k0 + IMG * (1 - a), IMG)
            for bi in range(3):
                moved = ext_ref[bi, :, pl.ds(start, TK)]
                acc_ref[ai * 3 + bi] += lax.dot_general(
                    tile, moved, (((1,), (1,)), ((), ())), preferred_element_type=jnp.float32
                )
        return carry

    lax.fori_loop(0, pix // TK, products, 0)

    scale = scale_ref[...]
    half_energy = 0.5 * energy_ref[...]
    scores = [scale * (acc_ref[t] - half_energy) for t in range(9)]
    highest = jnp.max(scores[0], axis=0, keepdims=True)
    for t in range(1, 9):
        highest = jnp.maximum(highest, jnp.max(scores[t], axis=0, keepdims=True))
    total = jnp.sum(jnp.exp(scores[0] - highest), axis=0, keepdims=True)
    for t in range(1, 9):
        total = total + jnp.sum(jnp.exp(scores[t] - highest), axis=0, keepdims=True)
    evidence = highest + jnp.log(total)
    evid_ref[...] = evidence
    gain = gain_ref[...]
    gain_hi = gain.astype(jnp.bfloat16)
    gain_lo = (gain - gain_hi.astype(jnp.float32)).astype(jnp.bfloat16)
    depth = gain.shape[0]
    for t in range(9):
        weights = jnp.exp(scores[t] - evidence).astype(jnp.bfloat16)
        mixed = jnp.dot(gain_hi, weights, preferred_element_type=jnp.float32) + jnp.dot(
            gain_lo, weights, preferred_element_type=jnp.float32
        )
        mixed_hi = mixed.astype(jnp.bfloat16).astype(jnp.float32)
        v_ref[t, 0:depth] = mixed_hi
        v_ref[t, depth:2 * depth] = mixed - mixed_hi

    band = pix // groups
    width = band // IMG

    def plane_tiles(j, carry):
        n0 = pl.multiple_of(j * band, band)
        summed = jnp.zeros((2 * depth, band), jnp.float32)
        for ai, a in enumerate(SHIFTS):
            start = pl.multiple_of(n0 + IMG * (1 - a), IMG)
            for bi in range(3):
                summed = summed + jnp.dot(
                    v_ref[ai * 3 + bi].astype(jnp.bfloat16), ext_ref[bi, :, pl.ds(start, band)],
                    preferred_element_type=jnp.float32,
                )
        plane = summed[0:depth] + summed[depth:2 * depth]
        before = lax.rem(j + groups - 1, groups)
        for z in range(depth):
            for u in range(width):
                row = z * (width + 1) + u
                planes_ref[j, pl.ds(row, 1), :] = plane[z:z + 1, u * IMG:(u + 1) * IMG]
            row = z * (width + 1) + width
            planes_ref[before, pl.ds(row, 1), :] = plane[z:z + 1, 0:IMG]
        return carry

    lax.fori_loop(0, groups, plane_tiles, 0)


def class_pass(rows_ext, templates, scale_row, energy_col, gain, pix, groups):
    rowcount = rows_ext.shape[0]
    refcount = templates.shape[0]
    depth = gain.shape[0]
    vmem = pl.BlockSpec(memory_space=pltpu.VMEM)
    flops = 2 * 9 * (refcount + 2 * depth) * rowcount * pix
    cost = pl.CostEstimate(
        flops=flops, transcendentals=10 * refcount * rowcount,
        bytes_accessed=rows_ext.size * 2 + templates.size * 2 + depth * pix * 4,
    )
    return pl.pallas_call(
        functools.partial(class_kernel, pix, groups),
        out_shape=(
            jax.ShapeDtypeStruct((groups, depth * (pix // groups // IMG + 1), IMG), jnp.float32),
            jax.ShapeDtypeStruct((1, rowcount), jnp.float32),
        ),
        in_specs=[vmem] * 5,
        out_specs=(vmem, vmem),
        scratch_shapes=[
            pltpu.VMEM((3, rowcount, pix + 2 * IMG), jnp.bfloat16),
            pltpu.VMEM((9, refcount, rowcount), jnp.float32),
            pltpu.VMEM((9, 2 * depth, rowcount), jnp.float32),
        ],
        compiler_params=pltpu.CompilerParams(vmem_limit_bytes=48 * 1024 * 1024),
        cost_estimate=cost,
    )(rows_ext, templates, scale_row, energy_col, gain)


def on_device(
    particles, particle_precision, particle_class, class_owner, references, insert_weights
):
    sources = lax.axis_size("dev")
    groups = lax.axis_size("grp")
    local_count, pix = particles.shape
    classes = class_owner.shape[0]
    owned_classes = references.shape[0]
    slot_depth = max(2, 2 * local_count // classes)
    labels = particle_class[:, 0]
    catalog = jnp.arange(classes, dtype=jnp.int32)
    position = jnp.sum(
        jnp.where(labels[:, None] == catalog[None, :], class_owner[None, :], 0), axis=1
    )
    ordinal = jnp.arange(local_count, dtype=jnp.int32)
    earlier = (labels[:, None] == labels[None, :]) & (ordinal[None, :] < ordinal[:, None])
    arrival = jnp.sum(earlier, axis=1)
    slot_index = arrival * classes + position
    total_slots = classes * slot_depth
    placing = (jnp.arange(total_slots, dtype=jnp.int32)[:, None] == slot_index[None, :]).astype(
        jnp.bfloat16
    )
    extra = jnp.broadcast_to(particle_precision[:, None], (local_count, IMG))
    carried = jnp.concatenate([particles, extra], axis=1)
    width = pix + IMG
    outgoing = jnp.dot(placing, carried, preferred_element_type=jnp.float32).astype(jnp.bfloat16)
    outgoing = outgoing.reshape(slot_depth, sources, owned_classes * width)
    arrived = lax.all_to_all(outgoing, "dev", split_axis=1, concat_axis=1, tiled=True)
    rows_ext = arrived.reshape(slot_depth * sources, width)
    scale_row = rows_ext[:, pix].astype(jnp.float32).reshape(1, slot_depth * sources)
    templates = references[0]
    energy_col = jnp.sum(jnp.square(templates.astype(jnp.float32)), axis=1).reshape(-1, 1)
    windows, class_evidence = class_pass(
        rows_ext, templates, scale_row, energy_col, insert_weights, pix, groups
    )
    stacked = class_evidence.reshape(slot_depth, sources)
    returned = lax.all_to_all(stacked, "dev", split_axis=1, concat_axis=1, tiled=True).reshape(
        total_slots
    )
    particle_evidence = jnp.take(returned, slot_index)
    depth = insert_weights.shape[0]
    band = IMG // groups
    mine = jnp.sum(lax.all_to_all(windows, "grp", split_axis=0, concat_axis=0, tiled=True), 0)
    mine = mine.reshape(depth, band + 1, IMG)
    interp = upsample_table(VOL, IMG)
    across = jnp.einsum("zjv,xv->zjx", mine, interp, precision=lax.Precision.HIGHEST)
    rows_table = local_table(2 * band, band + 1)
    volume = jnp.einsum("yj,zjx->yzx", rows_table, across, precision=lax.Precision.HIGHEST)
    return (volume, particle_evidence)


def solution(mesh):
    placed = (
        P(("grp", "dev"), None),
        P(("grp", "dev")),
        P(("grp", "dev"), None),
        P(),
        P("dev", None, None),
        P("dev", None),
    )
    return jax.shard_map(
        on_device,
        mesh=mesh,
        in_specs=placed,
        out_specs=(P("grp", "dev", None), P(("grp", "dev"))),
        check_vma=False,
    )
```

```python
import functools

import jax
import jax.numpy as jnp
from jax import lax
from jax.experimental import pallas as pl
from jax.experimental.pallas import tpu as pltpu
from jax.sharding import PartitionSpec as P

IMG = 128
VOL = 256
SHIFTS = (-1, 0, 1)
TK = 2048
TN = 1024


def upsample_table(length, source):
    target = jnp.arange(length, dtype=jnp.int32)[:, None]
    anchor = jnp.arange(source, dtype=jnp.int32)[None, :]
    halves = target // 2
    lower = anchor == halves
    upper = anchor == (halves + 1) % source
    is_even = target % 2 == 0
    even_part = jnp.where(lower, 1.0, 0.0)
    odd_part = jnp.where(lower, 0.5, 0.0) + jnp.where(upper, 0.5, 0.0)
    return jnp.where(is_even, even_part, odd_part).astype(jnp.float32)


def local_table(rows, anchors):
    target = jnp.arange(rows, dtype=jnp.int32)[:, None]
    anchor = jnp.arange(anchors, dtype=jnp.int32)[None, :]
    halves = target // 2
    lower = anchor == halves
    upper = anchor == halves + 1
    is_even = target % 2 == 0
    even_part = jnp.where(lower, 1.0, 0.0)
    odd_part = jnp.where(lower, 0.5, 0.0) + jnp.where(upper, 0.5, 0.0)
    return jnp.where(is_even, even_part, odd_part).astype(jnp.float32)


def class_kernel(pix, groups, rows_ref, ref_ref, scale_ref, energy_ref, gain_ref, planes_ref, evid_ref,
                 ext_ref, acc_ref, v_ref):
    chunks = pix // IMG

    def build(u, carry):
        off = pl.multiple_of(u * IMG, IMG)
        dst = pl.multiple_of(off + IMG, IMG)
        chunk = rows_ref[:, pl.ds(off, IMG)]
        wide = chunk.astype(jnp.float32)
        ext_ref[0, :, pl.ds(dst, IMG)] = pltpu.roll(wide, IMG - 1, 1).astype(jnp.bfloat16)
        ext_ref[1, :, pl.ds(dst, IMG)] = chunk
        ext_ref[2, :, pl.ds(dst, IMG)] = pltpu.roll(wide, 1, 1).astype(jnp.bfloat16)
        return carry

    lax.fori_loop(0, chunks, build, 0, unroll=8)
    ext_ref[:, :, 0:IMG] = ext_ref[:, :, pix:pix + IMG]
    ext_ref[:, :, pix + IMG:pix + 2 * IMG] = ext_ref[:, :, IMG:2 * IMG]

    acc_ref[...] = jnp.zeros_like(acc_ref)

    def products(j, carry):
        k0 = pl.multiple_of(j * TK, TK)
        tile = ref_ref[:, pl.ds(k0, TK)]
        for ai, a in enumerate(SHIFTS):
            start = pl.multiple_of(k0 + IMG * (1 - a), IMG)
            for bi in range(3):
                moved = ext_ref[bi, :, pl.ds(start, TK)]
                acc_ref[ai * 3 + bi] += lax.dot_general(
                    tile, moved, (((1,), (1,)), ((), ())), preferred_element_type=jnp.float32
                )
        return carry

    lax.fori_loop(0, pix // TK, products, 0)

    scale = scale_ref[...]
    half_energy = 0.5 * energy_ref[...]
    scores = [scale * (acc_ref[t] - half_energy) for t in range(9)]
    highest = jnp.max(scores[0], axis=0, keepdims=True)
    for t in range(1, 9):
        highest = jnp.maximum(highest, jnp.max(scores[t], axis=0, keepdims=True))
    total = jnp.sum(jnp.exp(scores[0] - highest), axis=0, keepdims=True)
    for t in range(1, 9):
        total = total + jnp.sum(jnp.exp(scores[t] - highest), axis=0, keepdims=True)
    evidence = highest + jnp.log(total)
    evid_ref[...] = evidence
    gain = gain_ref[...]
    gain_hi = gain.astype(jnp.bfloat16)
    gain_lo = (gain - gain_hi.astype(jnp.float32)).astype(jnp.bfloat16)
    depth = gain.shape[0]
    for t in range(9):
        weights = jnp.exp(scores[t] - evidence).astype(jnp.bfloat16)
        mixed = jnp.dot(gain_hi, weights, preferred_element_type=jnp.float32) + jnp.dot(
            gain_lo, weights, preferred_element_type=jnp.float32
        )
        mixed_hi = mixed.astype(jnp.bfloat16).astype(jnp.float32)
        v_ref[t, 0:depth] = mixed_hi
        v_ref[t, depth:2 * depth] = mixed - mixed_hi

    band = pix // groups
    width = band // IMG

    def plane_tiles(j, carry):
        n0 = pl.multiple_of(j * band, band)
        summed = jnp.zeros((2 * depth, band), jnp.float32)
        for ai, a in enumerate(SHIFTS):
            start = pl.multiple_of(n0 + IMG * (1 - a), IMG)
            for bi in range(3):
                summed = summed + jnp.dot(
                    v_ref[ai * 3 + bi].astype(jnp.bfloat16), ext_ref[bi, :, pl.ds(start, band)],
                    preferred_element_type=jnp.float32,
                )
        plane = summed[0:depth] + summed[depth:2 * depth]
        before = lax.rem(j + groups - 1, groups)
        for z in range(depth):
            for u in range(width):
                row = z * (width + 1) + u
                planes_ref[j, pl.ds(row, 1), :] = plane[z:z + 1, u * IMG:(u + 1) * IMG]
            row = z * (width + 1) + width
            planes_ref[before, pl.ds(row, 1), :] = plane[z:z + 1, 0:IMG]
        return carry

    lax.fori_loop(0, groups, plane_tiles, 0)


def class_pass(rows_ext, templates, scale_row, energy_col, gain, pix, groups):
    rowcount = rows_ext.shape[0]
    refcount = templates.shape[0]
    depth = gain.shape[0]
    vmem = pl.BlockSpec(memory_space=pltpu.VMEM)
    flops = 2 * 9 * (refcount + 2 * depth) * rowcount * pix
    cost = pl.CostEstimate(
        flops=flops, transcendentals=10 * refcount * rowcount,
        bytes_accessed=rows_ext.size * 2 + templates.size * 2 + depth * pix * 4,
    )
    return pl.pallas_call(
        functools.partial(class_kernel, pix, groups),
        out_shape=(
            jax.ShapeDtypeStruct((groups, depth * (pix // groups // IMG + 1), IMG), jnp.float32),
            jax.ShapeDtypeStruct((1, rowcount), jnp.float32),
        ),
        in_specs=[vmem] * 5,
        out_specs=(vmem, vmem),
        scratch_shapes=[
            pltpu.VMEM((3, rowcount, pix + 2 * IMG), jnp.bfloat16),
            pltpu.VMEM((9, refcount, rowcount), jnp.float32),
            pltpu.VMEM((9, 2 * depth, rowcount), jnp.float32),
        ],
        compiler_params=pltpu.CompilerParams(vmem_limit_bytes=48 * 1024 * 1024),
        cost_estimate=cost,
    )(rows_ext, templates, scale_row, energy_col, gain)


def on_device(
    particles, particle_precision, particle_class, class_owner, references, insert_weights
):
    sources = lax.axis_size("dev")
    groups = lax.axis_size("grp")
    local_count, pix = particles.shape
    classes = class_owner.shape[0]
    owned_classes = references.shape[0]
    slot_depth = max(2, 2 * local_count // classes)
    labels = particle_class[:, 0]
    catalog = jnp.arange(classes, dtype=jnp.int32)
    position = jnp.sum(
        jnp.where(labels[:, None] == catalog[None, :], class_owner[None, :], 0), axis=1
    )
    ordinal = jnp.arange(local_count, dtype=jnp.int32)
    earlier = (labels[:, None] == labels[None, :]) & (ordinal[None, :] < ordinal[:, None])
    arrival = jnp.sum(earlier, axis=1)
    slot_index = arrival * classes + position
    total_slots = classes * slot_depth
    placing = (jnp.arange(total_slots, dtype=jnp.int32)[:, None] == slot_index[None, :]).astype(
        jnp.bfloat16
    )
    extra = jnp.broadcast_to(particle_precision[:, None], (local_count, IMG))
    carried = jnp.concatenate([particles, extra], axis=1)
    width = pix + IMG
    outgoing = jnp.dot(placing, carried, preferred_element_type=jnp.float32).astype(jnp.bfloat16)
    outgoing = outgoing.reshape(slot_depth, sources, owned_classes * width)
    arrived = lax.all_to_all(outgoing, "dev", split_axis=1, concat_axis=1, tiled=True)
    rows_ext = arrived.reshape(slot_depth * sources, width)
    scale_row = rows_ext[:, pix].astype(jnp.float32).reshape(1, slot_depth * sources)
    templates = references[0]
    energy_col = jnp.sum(jnp.square(templates.astype(jnp.float32)), axis=1).reshape(-1, 1)
    windows, class_evidence = class_pass(
        rows_ext, templates, scale_row, energy_col, insert_weights, pix, groups
    )
    gathered = lax.all_gather(class_evidence.reshape(total_slots), "dev", tiled=True)
    me = lax.axis_index("dev")
    particle_evidence = jnp.take(gathered, position * total_slots + arrival * sources + me)
    depth = insert_weights.shape[0]
    band = IMG // groups
    mine = jnp.sum(lax.all_to_all(windows, "grp", split_axis=0, concat_axis=0, tiled=True), 0)
    mine = mine.reshape(depth, band + 1, IMG)
    interp = upsample_table(VOL, IMG)
    across = jnp.einsum("zjv,xv->zjx", mine, interp, precision=lax.Precision.HIGHEST)
    rows_table = local_table(2 * band, band + 1)
    volume = jnp.einsum("yj,zjx->yzx", rows_table, across, precision=lax.Precision.HIGHEST)
    return (volume, particle_evidence)


def solution(mesh):
    placed = (
        P(("grp", "dev"), None),
        P(("grp", "dev")),
        P(("grp", "dev"), None),
        P(),
        P("dev", None, None),
        P("dev", None),
    )
    return jax.shard_map(
        on_device,
        mesh=mesh,
        in_specs=placed,
        out_specs=(P("grp", "dev", None), P(("grp", "dev"))),
        check_vma=False,
    )
```

```python
import functools

import jax
import jax.numpy as jnp
from jax import lax
from jax.experimental import pallas as pl
from jax.experimental.pallas import tpu as pltpu
from jax.sharding import PartitionSpec as P

IMG = 128
VOL = 256
SHIFTS = (-1, 0, 1)
TK = 2048
TN = 1024


def upsample_table(length, source):
    target = jnp.arange(length, dtype=jnp.int32)[:, None]
    anchor = jnp.arange(source, dtype=jnp.int32)[None, :]
    halves = target // 2
    lower = anchor == halves
    upper = anchor == (halves + 1) % source
    is_even = target % 2 == 0
    even_part = jnp.where(lower, 1.0, 0.0)
    odd_part = jnp.where(lower, 0.5, 0.0) + jnp.where(upper, 0.5, 0.0)
    return jnp.where(is_even, even_part, odd_part).astype(jnp.float32)


def local_table(rows, anchors):
    target = jnp.arange(rows, dtype=jnp.int32)[:, None]
    anchor = jnp.arange(anchors, dtype=jnp.int32)[None, :]
    halves = target // 2
    lower = anchor == halves
    upper = anchor == halves + 1
    is_even = target % 2 == 0
    even_part = jnp.where(lower, 1.0, 0.0)
    odd_part = jnp.where(lower, 0.5, 0.0) + jnp.where(upper, 0.5, 0.0)
    return jnp.where(is_even, even_part, odd_part).astype(jnp.float32)


def class_kernel(pix, groups, rows_ref, ref_ref, scale_ref, energy_ref, gain_ref, planes_ref, evid_ref,
                 ext_ref, acc_ref, v_ref):
    chunks = pix // IMG

    def build(u, carry):
        off = pl.multiple_of(u * IMG, IMG)
        dst = pl.multiple_of(off + IMG, IMG)
        chunk = rows_ref[:, pl.ds(off, IMG)]
        wide = chunk.astype(jnp.float32)
        ext_ref[0, :, pl.ds(dst, IMG)] = pltpu.roll(wide, IMG - 1, 1).astype(jnp.bfloat16)
        ext_ref[1, :, pl.ds(dst, IMG)] = chunk
        ext_ref[2, :, pl.ds(dst, IMG)] = pltpu.roll(wide, 1, 1).astype(jnp.bfloat16)
        return carry

    lax.fori_loop(0, chunks, build, 0, unroll=8)
    ext_ref[:, :, 0:IMG] = ext_ref[:, :, pix:pix + IMG]
    ext_ref[:, :, pix + IMG:pix + 2 * IMG] = ext_ref[:, :, IMG:2 * IMG]

    acc_ref[...] = jnp.zeros_like(acc_ref)

    def products(j, carry):
        k0 = pl.multiple_of(j * TK, TK)
        tile = ref_ref[:, pl.ds(k0, TK)]
        for ai, a in enumerate(SHIFTS):
            start = pl.multiple_of(k0 + IMG * (1 - a), IMG)
            for bi in range(3):
                moved = ext_ref[bi, :, pl.ds(start, TK)]
                acc_ref[ai * 3 + bi] += lax.dot_general(
                    tile, moved, (((1,), (1,)), ((), ())), preferred_element_type=jnp.float32
                )
        return carry

    lax.fori_loop(0, pix // TK, products, 0)

    scale = scale_ref[...]
    half_energy = 0.5 * energy_ref[...]
    scores = [scale * (acc_ref[t] - half_energy) for t in range(9)]
    highest = jnp.max(scores[0], axis=0, keepdims=True)
    for t in range(1, 9):
        highest = jnp.maximum(highest, jnp.max(scores[t], axis=0, keepdims=True))
    total = jnp.sum(jnp.exp(scores[0] - highest), axis=0, keepdims=True)
    for t in range(1, 9):
        total = total + jnp.sum(jnp.exp(scores[t] - highest), axis=0, keepdims=True)
    evidence = highest + jnp.log(total)
    evid_ref[...] = evidence
    gain = gain_ref[...]
    gain_hi = gain.astype(jnp.bfloat16)
    gain_lo = (gain - gain_hi.astype(jnp.float32)).astype(jnp.bfloat16)
    depth = gain.shape[0]
    for t in range(9):
        weights = jnp.exp(scores[t] - evidence).astype(jnp.bfloat16)
        mixed = jnp.dot(gain_hi, weights, preferred_element_type=jnp.float32) + jnp.dot(
            gain_lo, weights, preferred_element_type=jnp.float32
        )
        mixed_hi = mixed.astype(jnp.bfloat16).astype(jnp.float32)
        v_ref[t, 0:depth] = mixed_hi
        v_ref[t, depth:2 * depth] = mixed - mixed_hi

    band = pix // groups
    width = band // IMG

    def plane_tiles(j, carry):
        n0 = pl.multiple_of(j * band, band)
        summed = jnp.zeros((2 * depth, band), jnp.float32)
        for ai, a in enumerate(SHIFTS):
            start = pl.multiple_of(n0 + IMG * (1 - a), IMG)
            for bi in range(3):
                summed = summed + jnp.dot(
                    v_ref[ai * 3 + bi].astype(jnp.bfloat16), ext_ref[bi, :, pl.ds(start, band)],
                    preferred_element_type=jnp.float32,
                )
        plane = summed[0:depth] + summed[depth:2 * depth]
        before = lax.rem(j + groups - 1, groups)
        for z in range(depth):
            for u in range(width):
                row = z * (width + 1) + u
                planes_ref[j, pl.ds(row, 1), :] = plane[z:z + 1, u * IMG:(u + 1) * IMG]
            row = z * (width + 1) + width
            planes_ref[before, pl.ds(row, 1), :] = plane[z:z + 1, 0:IMG]
        return carry

    lax.fori_loop(0, groups, plane_tiles, 0)


def class_pass(rows_ext, templates, scale_row, energy_col, gain, pix, groups):
    rowcount = rows_ext.shape[0]
    refcount = templates.shape[0]
    depth = gain.shape[0]
    vmem = pl.BlockSpec(memory_space=pltpu.VMEM)
    flops = 2 * 9 * (refcount + 2 * depth) * rowcount * pix
    cost = pl.CostEstimate(
        flops=flops, transcendentals=10 * refcount * rowcount,
        bytes_accessed=rows_ext.size * 2 + templates.size * 2 + depth * pix * 4,
    )
    return pl.pallas_call(
        functools.partial(class_kernel, pix, groups),
        out_shape=(
            jax.ShapeDtypeStruct((groups, depth * (pix // groups // IMG + 1), IMG), jnp.float32),
            jax.ShapeDtypeStruct((1, rowcount), jnp.float32),
        ),
        in_specs=[vmem] * 5,
        out_specs=(vmem, vmem),
        scratch_shapes=[
            pltpu.VMEM((3, rowcount, pix + 2 * IMG), jnp.bfloat16),
            pltpu.VMEM((9, refcount, rowcount), jnp.float32),
            pltpu.VMEM((9, 2 * depth, rowcount), jnp.float32),
        ],
        compiler_params=pltpu.CompilerParams(vmem_limit_bytes=48 * 1024 * 1024),
        cost_estimate=cost,
    )(rows_ext, templates, scale_row, energy_col, gain)


def on_device(
    particles, particle_precision, particle_class, class_owner, references, insert_weights
):
    sources = lax.axis_size("dev")
    groups = lax.axis_size("grp")
    local_count, pix = particles.shape
    classes = class_owner.shape[0]
    owned_classes = references.shape[0]
    slot_depth = max(2, 2 * local_count // classes)
    labels = particle_class[:, 0]
    catalog = jnp.arange(classes, dtype=jnp.int32)
    position = jnp.sum(
        jnp.where(labels[:, None] == catalog[None, :], class_owner[None, :], 0), axis=1
    )
    ordinal = jnp.arange(local_count, dtype=jnp.int32)
    earlier = (labels[:, None] == labels[None, :]) & (ordinal[None, :] < ordinal[:, None])
    arrival = jnp.sum(earlier, axis=1)
    slot_index = arrival * classes + position
    total_slots = classes * slot_depth
    placing = (jnp.arange(total_slots, dtype=jnp.int32)[:, None] == slot_index[None, :]).astype(
        jnp.bfloat16
    )
    extra = jnp.broadcast_to(particle_precision[:, None], (local_count, IMG))
    carried = jnp.concatenate([particles, extra], axis=1)
    width = pix + IMG
    outgoing = jnp.dot(placing, carried, preferred_element_type=jnp.float32).astype(jnp.bfloat16)
    outgoing = outgoing.reshape(slot_depth, sources, owned_classes * width)
    arrived = lax.all_to_all(outgoing, "dev", split_axis=1, concat_axis=1, tiled=True)
    rows_ext = arrived.reshape(slot_depth * sources, width)
    scale_row = rows_ext[:, pix].astype(jnp.float32).reshape(1, slot_depth * sources)
    templates = references[0]
    energy_col = jnp.sum(jnp.square(templates.astype(jnp.float32)), axis=1).reshape(-1, 1)
    windows, class_evidence = class_pass(
        rows_ext, templates, scale_row, energy_col, insert_weights, pix, groups
    )
    stacked = class_evidence.reshape(slot_depth, sources)
    returned = lax.all_to_all(stacked, "dev", split_axis=1, concat_axis=1, tiled=True).reshape(
        total_slots
    )
    particle_evidence = jnp.take(returned, slot_index)
    depth = insert_weights.shape[0]
    band = IMG // groups
    here = lax.axis_index("grp")
    mine = lax.dynamic_index_in_dim(windows, here, 0, keepdims=False)
    for step in range(1, groups):
        part = lax.dynamic_index_in_dim(windows, lax.rem(here + step, groups), 0, keepdims=False)
        pairs = [(g, (g + step) % groups) for g in range(groups)]
        mine = mine + lax.ppermute(part, "grp", pairs)
    mine = mine.reshape(depth, band + 1, IMG)
    interp = upsample_table(VOL, IMG)
    across = jnp.einsum("zjv,xv->zjx", mine, interp, precision=lax.Precision.HIGHEST)
    rows_table = local_table(2 * band, band + 1)
    volume = jnp.einsum("yj,zjx->yzx", rows_table, across, precision=lax.Precision.HIGHEST)
    return (volume, particle_evidence)


def solution(mesh):
    placed = (
        P(("grp", "dev"), None),
        P(("grp", "dev")),
        P(("grp", "dev"), None),
        P(),
        P("dev", None, None),
        P("dev", None),
    )
    return jax.shard_map(
        on_device,
        mesh=mesh,
        in_specs=placed,
        out_specs=(P("grp", "dev", None), P(("grp", "dev"))),
        check_vma=False,
    )
```

```python
import functools

import jax
import jax.numpy as jnp
from jax import lax
from jax.experimental import pallas as pl
from jax.experimental.pallas import tpu as pltpu
from jax.sharding import PartitionSpec as P

IMG = 128
VOL = 256
SHIFTS = (-1, 0, 1)
TK = 2048
TN = 1024


def upsample_table(length, source):
    target = jnp.arange(length, dtype=jnp.int32)[:, None]
    anchor = jnp.arange(source, dtype=jnp.int32)[None, :]
    halves = target // 2
    lower = anchor == halves
    upper = anchor == (halves + 1) % source
    is_even = target % 2 == 0
    even_part = jnp.where(lower, 1.0, 0.0)
    odd_part = jnp.where(lower, 0.5, 0.0) + jnp.where(upper, 0.5, 0.0)
    return jnp.where(is_even, even_part, odd_part).astype(jnp.float32)


def local_table(rows, anchors):
    target = jnp.arange(rows, dtype=jnp.int32)[:, None]
    anchor = jnp.arange(anchors, dtype=jnp.int32)[None, :]
    halves = target // 2
    lower = anchor == halves
    upper = anchor == halves + 1
    is_even = target % 2 == 0
    even_part = jnp.where(lower, 1.0, 0.0)
    odd_part = jnp.where(lower, 0.5, 0.0) + jnp.where(upper, 0.5, 0.0)
    return jnp.where(is_even, even_part, odd_part).astype(jnp.float32)


def class_kernel(pix, groups, rows_ref, ref_ref, scale_ref, energy_ref, gain_ref, planes_ref, evid_ref,
                 ext_ref, acc_ref, v_ref):
    chunks = pix // IMG

    def build(u, carry):
        off = pl.multiple_of(u * IMG, IMG)
        dst = pl.multiple_of(off + IMG, IMG)
        chunk = rows_ref[:, pl.ds(off, IMG)]
        wide = chunk.astype(jnp.float32)
        ext_ref[0, :, pl.ds(dst, IMG)] = pltpu.roll(wide, IMG - 1, 1).astype(jnp.bfloat16)
        ext_ref[1, :, pl.ds(dst, IMG)] = chunk
        ext_ref[2, :, pl.ds(dst, IMG)] = pltpu.roll(wide, 1, 1).astype(jnp.bfloat16)
        return carry

    lax.fori_loop(0, chunks, build, 0, unroll=8)
    ext_ref[:, :, 0:IMG] = ext_ref[:, :, pix:pix + IMG]
    ext_ref[:, :, pix + IMG:pix + 2 * IMG] = ext_ref[:, :, IMG:2 * IMG]

    acc_ref[...] = jnp.zeros_like(acc_ref)

    def products(j, carry):
        k0 = pl.multiple_of(j * TK, TK)
        tile = ref_ref[:, pl.ds(k0, TK)]
        for ai, a in enumerate(SHIFTS):
            start = pl.multiple_of(k0 + IMG * (1 - a), IMG)
            for bi in range(3):
                moved = ext_ref[bi, :, pl.ds(start, TK)]
                acc_ref[ai * 3 + bi] += lax.dot_general(
                    tile, moved, (((1,), (1,)), ((), ())), preferred_element_type=jnp.float32
                )
        return carry

    lax.fori_loop(0, pix // TK, products, 0)

    scale = scale_ref[...]
    half_energy = 0.5 * energy_ref[...]
    scores = [scale * (acc_ref[t] - half_energy) for t in range(9)]
    highest = jnp.max(scores[0], axis=0, keepdims=True)
    for t in range(1, 9):
        highest = jnp.maximum(highest, jnp.max(scores[t], axis=0, keepdims=True))
    total = jnp.sum(jnp.exp(scores[0] - highest), axis=0, keepdims=True)
    for t in range(1, 9):
        total = total + jnp.sum(jnp.exp(scores[t] - highest), axis=0, keepdims=True)
    evidence = highest + jnp.log(total)
    evid_ref[...] = evidence
    gain = gain_ref[...]
    gain_hi = gain.astype(jnp.bfloat16)
    gain_lo = (gain - gain_hi.astype(jnp.float32)).astype(jnp.bfloat16)
    depth = gain.shape[0]
    for t in range(9):
        weights = jnp.exp(scores[t] - evidence).astype(jnp.bfloat16)
        mixed = jnp.dot(gain_hi, weights, preferred_element_type=jnp.float32) + jnp.dot(
            gain_lo, weights, preferred_element_type=jnp.float32
        )
        mixed_hi = mixed.astype(jnp.bfloat16).astype(jnp.float32)
        v_ref[t, 0:depth] = mixed_hi
        v_ref[t, depth:2 * depth] = mixed - mixed_hi

    band = pix // groups
    width = band // IMG

    def plane_tiles(j, carry):
        n0 = pl.multiple_of(j * band, band)
        summed = jnp.zeros((2 * depth, band), jnp.float32)
        for ai, a in enumerate(SHIFTS):
            start = pl.multiple_of(n0 + IMG * (1 - a), IMG)
            for bi in range(3):
                summed = summed + jnp.dot(
                    v_ref[ai * 3 + bi].astype(jnp.bfloat16), ext_ref[bi, :, pl.ds(start, band)],
                    preferred_element_type=jnp.float32,
                )
        plane = summed[0:depth] + summed[depth:2 * depth]
        before = lax.rem(j + groups - 1, groups)
        for z in range(depth):
            for u in range(width):
                row = z * (width + 1) + u
                planes_ref[j, pl.ds(row, 1), :] = plane[z:z + 1, u * IMG:(u + 1) * IMG]
            row = z * (width + 1) + width
            planes_ref[before, pl.ds(row, 1), :] = plane[z:z + 1, 0:IMG]
        return carry

    lax.fori_loop(0, groups, plane_tiles, 0)


def class_pass(rows_ext, templates, scale_row, energy_col, gain, pix, groups):
    rowcount = rows_ext.shape[0]
    refcount = templates.shape[0]
    depth = gain.shape[0]
    vmem = pl.BlockSpec(memory_space=pltpu.VMEM)
    flops = 2 * 9 * (refcount + 2 * depth) * rowcount * pix
    cost = pl.CostEstimate(
        flops=flops, transcendentals=10 * refcount * rowcount,
        bytes_accessed=rows_ext.size * 2 + templates.size * 2 + depth * pix * 4,
    )
    return pl.pallas_call(
        functools.partial(class_kernel, pix, groups),
        out_shape=(
            jax.ShapeDtypeStruct((groups, depth * (pix // groups // IMG + 1), IMG), jnp.float32),
            jax.ShapeDtypeStruct((1, rowcount), jnp.float32),
        ),
        in_specs=[vmem] * 5,
        out_specs=(vmem, vmem),
        scratch_shapes=[
            pltpu.VMEM((3, rowcount, pix + 2 * IMG), jnp.bfloat16),
            pltpu.VMEM((9, refcount, rowcount), jnp.float32),
            pltpu.VMEM((9, 2 * depth, rowcount), jnp.float32),
        ],
        compiler_params=pltpu.CompilerParams(vmem_limit_bytes=48 * 1024 * 1024),
        cost_estimate=cost,
    )(rows_ext, templates, scale_row, energy_col, gain)


def on_device(
    particles, particle_precision, particle_class, class_owner, references, insert_weights
):
    sources = lax.axis_size("dev")
    groups = lax.axis_size("grp")
    local_count, pix = particles.shape
    classes = class_owner.shape[0]
    owned_classes = references.shape[0]
    slot_depth = max(2, 2 * local_count // classes)
    labels = particle_class[:, 0]
    catalog = jnp.arange(classes, dtype=jnp.int32)
    position = jnp.sum(
        jnp.where(labels[:, None] == catalog[None, :], class_owner[None, :], 0), axis=1
    )
    ordinal = jnp.arange(local_count, dtype=jnp.int32)
    earlier = (labels[:, None] == labels[None, :]) & (ordinal[None, :] < ordinal[:, None])
    arrival = jnp.sum(earlier, axis=1)
    me = lax.axis_index("dev")
    relative = lax.rem(position - me + sources, sources)
    slot_index = relative * slot_depth + arrival
    total_slots = classes * slot_depth
    placing = (jnp.arange(total_slots, dtype=jnp.int32)[:, None] == slot_index[None, :]).astype(
        jnp.bfloat16
    )
    extra = jnp.broadcast_to(particle_precision[:, None], (local_count, IMG))
    carried = jnp.concatenate([particles, extra], axis=1)
    width = pix + IMG
    outgoing = jnp.dot(placing, carried, preferred_element_type=jnp.float32).astype(jnp.bfloat16)
    outgoing = outgoing.reshape(sources, owned_classes * slot_depth, width)
    pieces = [outgoing[0]]
    for step in range(1, sources):
        pairs = [(d, (d + step) % sources) for d in range(sources)]
        pieces.append(lax.ppermute(outgoing[step], "dev", pairs))
    rows_ext = jnp.stack(pieces, 0).reshape(sources * slot_depth, width)
    scale_row = rows_ext[:, pix].astype(jnp.float32).reshape(1, sources * slot_depth)
    templates = references[0]
    energy_col = jnp.sum(jnp.square(templates.astype(jnp.float32)), axis=1).reshape(-1, 1)
    windows, class_evidence = class_pass(
        rows_ext, templates, scale_row, energy_col, insert_weights, pix, groups
    )
    by_step = class_evidence.reshape(sources, slot_depth)
    by_source = jnp.roll(jnp.flip(by_step, 0), me + 1, axis=0)
    returned = lax.all_to_all(by_source, "dev", split_axis=0, concat_axis=0, tiled=True).reshape(
        total_slots
    )
    particle_evidence = jnp.take(returned, position * slot_depth + arrival)
    depth = insert_weights.shape[0]
    band = IMG // groups
    here = lax.axis_index("grp")
    mine = lax.dynamic_index_in_dim(windows, here, 0, keepdims=False)
    for step in range(1, groups):
        part = lax.dynamic_index_in_dim(windows, lax.rem(here + step, groups), 0, keepdims=False)
        pairs = [(g, (g + step) % groups) for g in range(groups)]
        mine = mine + lax.ppermute(part, "grp", pairs)
    mine = mine.reshape(depth, band + 1, IMG)
    interp = upsample_table(VOL, IMG)
    across = jnp.einsum("zjv,xv->zjx", mine, interp, precision=lax.Precision.HIGHEST)
    rows_table = local_table(2 * band, band + 1)
    volume = jnp.einsum("yj,zjx->yzx", rows_table, across, precision=lax.Precision.HIGHEST)
    return (volume, particle_evidence)


def solution(mesh):
    placed = (
        P(("grp", "dev"), None),
        P(("grp", "dev")),
        P(("grp", "dev"), None),
        P(),
        P("dev", None, None),
        P("dev", None),
    )
    return jax.shard_map(
        on_device,
        mesh=mesh,
        in_specs=placed,
        out_specs=(P("grp", "dev", None), P(("grp", "dev"))),
        check_vma=False,
    )
```

```python
import functools

import jax
import jax.numpy as jnp
from jax import lax
from jax.experimental import pallas as pl
from jax.experimental.pallas import tpu as pltpu
from jax.sharding import PartitionSpec as P

IMG = 128
VOL = 256
SHIFTS = (-1, 0, 1)
TK = 2048
TN = 1024


def upsample_table(length, source):
    target = jnp.arange(length, dtype=jnp.int32)[:, None]
    anchor = jnp.arange(source, dtype=jnp.int32)[None, :]
    halves = target // 2
    lower = anchor == halves
    upper = anchor == (halves + 1) % source
    is_even = target % 2 == 0
    even_part = jnp.where(lower, 1.0, 0.0)
    odd_part = jnp.where(lower, 0.5, 0.0) + jnp.where(upper, 0.5, 0.0)
    return jnp.where(is_even, even_part, odd_part).astype(jnp.float32)


def local_table(rows, anchors):
    target = jnp.arange(rows, dtype=jnp.int32)[:, None]
    anchor = jnp.arange(anchors, dtype=jnp.int32)[None, :]
    halves = target // 2
    lower = anchor == halves
    upper = anchor == halves + 1
    is_even = target % 2 == 0
    even_part = jnp.where(lower, 1.0, 0.0)
    odd_part = jnp.where(lower, 0.5, 0.0) + jnp.where(upper, 0.5, 0.0)
    return jnp.where(is_even, even_part, odd_part).astype(jnp.float32)


def class_kernel(pix, groups, rows_ref, ref_ref, scale_ref, energy_ref, gain_ref, planes_ref, evid_ref,
                 ext_ref, acc_ref, v_ref):
    chunks = pix // IMG

    def build(u, carry):
        off = pl.multiple_of(u * IMG, IMG)
        dst = pl.multiple_of(off + IMG, IMG)
        chunk = rows_ref[:, pl.ds(off, IMG)]
        wide = chunk.astype(jnp.float32)
        ext_ref[0, :, pl.ds(dst, IMG)] = pltpu.roll(wide, IMG - 1, 1).astype(jnp.bfloat16)
        ext_ref[1, :, pl.ds(dst, IMG)] = chunk
        ext_ref[2, :, pl.ds(dst, IMG)] = pltpu.roll(wide, 1, 1).astype(jnp.bfloat16)
        return carry

    lax.fori_loop(0, chunks, build, 0, unroll=8)
    ext_ref[:, :, 0:IMG] = ext_ref[:, :, pix:pix + IMG]
    ext_ref[:, :, pix + IMG:pix + 2 * IMG] = ext_ref[:, :, IMG:2 * IMG]

    acc_ref[...] = jnp.zeros_like(acc_ref)

    def products(j, carry):
        k0 = pl.multiple_of(j * TK, TK)
        tile = ref_ref[pl.ds(k0, TK), :]
        for ai, a in enumerate(SHIFTS):
            start = pl.multiple_of(k0 + IMG * (1 - a), IMG)
            for bi in range(3):
                moved = ext_ref[bi, :, pl.ds(start, TK)]
                acc_ref[ai * 3 + bi] += jnp.dot(moved, tile, preferred_element_type=jnp.float32)
        return carry

    lax.fori_loop(0, pix // TK, products, 0)

    scale = scale_ref[...]
    half_energy = 0.5 * energy_ref[...]
    scores = [scale * (acc_ref[t] - half_energy) for t in range(9)]
    highest = jnp.max(scores[0], axis=1, keepdims=True)
    for t in range(1, 9):
        highest = jnp.maximum(highest, jnp.max(scores[t], axis=1, keepdims=True))
    total = jnp.sum(jnp.exp(scores[0] - highest), axis=1, keepdims=True)
    for t in range(1, 9):
        total = total + jnp.sum(jnp.exp(scores[t] - highest), axis=1, keepdims=True)
    evidence = highest + jnp.log(total)
    evid_ref[...] = evidence
    gain = gain_ref[...]
    gain_hi = gain.astype(jnp.bfloat16)
    gain_lo = (gain - gain_hi.astype(jnp.float32)).astype(jnp.bfloat16)
    depth = gain.shape[0]
    contract = (((1,), (1,)), ((), ()))
    for t in range(9):
        weights = jnp.exp(scores[t] - evidence).astype(jnp.bfloat16)
        mixed = lax.dot_general(
            gain_hi, weights, contract, preferred_element_type=jnp.float32
        ) + lax.dot_general(gain_lo, weights, contract, preferred_element_type=jnp.float32)
        mixed_hi = mixed.astype(jnp.bfloat16).astype(jnp.float32)
        v_ref[t, 0:depth] = mixed_hi
        v_ref[t, depth:2 * depth] = mixed - mixed_hi

    band = pix // groups
    width = band // IMG

    def plane_tiles(j, carry):
        n0 = pl.multiple_of(j * band, band)
        summed = jnp.zeros((2 * depth, band), jnp.float32)
        for ai, a in enumerate(SHIFTS):
            start = pl.multiple_of(n0 + IMG * (1 - a), IMG)
            for bi in range(3):
                summed = summed + jnp.dot(
                    v_ref[ai * 3 + bi].astype(jnp.bfloat16), ext_ref[bi, :, pl.ds(start, band)],
                    preferred_element_type=jnp.float32,
                )
        plane = summed[0:depth] + summed[depth:2 * depth]
        before = lax.rem(j + groups - 1, groups)
        for z in range(depth):
            for u in range(width):
                row = z * (width + 1) + u
                planes_ref[j, pl.ds(row, 1), :] = plane[z:z + 1, u * IMG:(u + 1) * IMG]
            row = z * (width + 1) + width
            planes_ref[before, pl.ds(row, 1), :] = plane[z:z + 1, 0:IMG]
        return carry

    lax.fori_loop(0, groups, plane_tiles, 0)


def class_pass(rows_ext, templates, scale_row, energy_col, gain, pix, groups):
    rowcount = rows_ext.shape[0]
    refcount = templates.shape[1]
    depth = gain.shape[0]
    vmem = pl.BlockSpec(memory_space=pltpu.VMEM)
    flops = 2 * 9 * (refcount + 2 * depth) * rowcount * pix
    cost = pl.CostEstimate(
        flops=flops, transcendentals=10 * refcount * rowcount,
        bytes_accessed=rows_ext.size * 2 + templates.size * 2 + depth * pix * 4,
    )
    return pl.pallas_call(
        functools.partial(class_kernel, pix, groups),
        out_shape=(
            jax.ShapeDtypeStruct((groups, depth * (pix // groups // IMG + 1), IMG), jnp.float32),
            jax.ShapeDtypeStruct((rowcount, 1), jnp.float32),
        ),
        in_specs=[vmem] * 5,
        out_specs=(vmem, vmem),
        scratch_shapes=[
            pltpu.VMEM((3, rowcount, pix + 2 * IMG), jnp.bfloat16),
            pltpu.VMEM((9, rowcount, refcount), jnp.float32),
            pltpu.VMEM((9, 2 * depth, rowcount), jnp.float32),
        ],
        compiler_params=pltpu.CompilerParams(vmem_limit_bytes=48 * 1024 * 1024),
        cost_estimate=cost,
    )(rows_ext, templates, scale_row, energy_col, gain)


def on_device(
    particles, particle_precision, particle_class, class_owner, references, insert_weights
):
    sources = lax.axis_size("dev")
    groups = lax.axis_size("grp")
    local_count, pix = particles.shape
    classes = class_owner.shape[0]
    owned_classes = references.shape[0]
    slot_depth = max(2, 2 * local_count // classes)
    labels = particle_class[:, 0]
    catalog = jnp.arange(classes, dtype=jnp.int32)
    position = jnp.sum(
        jnp.where(labels[:, None] == catalog[None, :], class_owner[None, :], 0), axis=1
    )
    ordinal = jnp.arange(local_count, dtype=jnp.int32)
    earlier = (labels[:, None] == labels[None, :]) & (ordinal[None, :] < ordinal[:, None])
    arrival = jnp.sum(earlier, axis=1)
    slot_index = arrival * classes + position
    total_slots = classes * slot_depth
    placing = (jnp.arange(total_slots, dtype=jnp.int32)[:, None] == slot_index[None, :]).astype(
        jnp.bfloat16
    )
    extra = jnp.broadcast_to(particle_precision[:, None], (local_count, IMG))
    carried = jnp.concatenate([particles, extra], axis=1)
    width = pix + IMG
    outgoing = jnp.dot(placing, carried, preferred_element_type=jnp.float32).astype(jnp.bfloat16)
    outgoing = outgoing.reshape(slot_depth, sources, owned_classes * width)
    arrived = lax.all_to_all(outgoing, "dev", split_axis=1, concat_axis=1, tiled=True)
    rows_ext = arrived.reshape(slot_depth * sources, width)
    scale_col = rows_ext[:, pix].astype(jnp.float32).reshape(slot_depth * sources, 1)
    templates = references[0]
    energy_row = jnp.sum(jnp.square(templates.astype(jnp.float32)), axis=1).reshape(1, -1)
    windows, class_evidence = class_pass(
        rows_ext, templates.T, scale_col, energy_row, insert_weights, pix, groups
    )
    stacked = class_evidence.reshape(slot_depth, sources)
    returned = lax.all_to_all(stacked, "dev", split_axis=1, concat_axis=1, tiled=True).reshape(
        total_slots
    )
    particle_evidence = jnp.take(returned, slot_index)
    depth = insert_weights.shape[0]
    band = IMG // groups
    here = lax.axis_index("grp")
    mine = lax.dynamic_index_in_dim(windows, here, 0, keepdims=False)
    for step in range(1, groups):
        part = lax.dynamic_index_in_dim(windows, lax.rem(here + step, groups), 0, keepdims=False)
        pairs = [(g, (g + step) % groups) for g in range(groups)]
        mine = mine + lax.ppermute(part, "grp", pairs)
    mine = mine.reshape(depth, band + 1, IMG)
    interp = upsample_table(VOL, IMG)
    across = jnp.einsum("zjv,xv->zjx", mine, interp, precision=lax.Precision.HIGHEST)
    rows_table = local_table(2 * band, band + 1)
    volume = jnp.einsum("yj,zjx->yzx", rows_table, across, precision=lax.Precision.HIGHEST)
    return (volume, particle_evidence)


def solution(mesh):
    placed = (
        P(("grp", "dev"), None),
        P(("grp", "dev")),
        P(("grp", "dev"), None),
        P(),
        P("dev", None, None),
        P("dev", None),
    )
    return jax.shard_map(
        on_device,
        mesh=mesh,
        in_specs=placed,
        out_specs=(P("grp", "dev", None), P(("grp", "dev"))),
        check_vma=False,
    )
```

```python
import functools

import jax
import jax.numpy as jnp
from jax import lax
from jax.experimental import pallas as pl
from jax.experimental.pallas import tpu as pltpu
from jax.sharding import PartitionSpec as P

IMG = 128
VOL = 256
SHIFTS = (-1, 0, 1)
TK = 2048
TN = 1024


def upsample_table(length, source):
    target = jnp.arange(length, dtype=jnp.int32)[:, None]
    anchor = jnp.arange(source, dtype=jnp.int32)[None, :]
    halves = target // 2
    lower = anchor == halves
    upper = anchor == (halves + 1) % source
    is_even = target % 2 == 0
    even_part = jnp.where(lower, 1.0, 0.0)
    odd_part = jnp.where(lower, 0.5, 0.0) + jnp.where(upper, 0.5, 0.0)
    return jnp.where(is_even, even_part, odd_part).astype(jnp.float32)


def local_table(rows, anchors):
    target = jnp.arange(rows, dtype=jnp.int32)[:, None]
    anchor = jnp.arange(anchors, dtype=jnp.int32)[None, :]
    halves = target // 2
    lower = anchor == halves
    upper = anchor == halves + 1
    is_even = target % 2 == 0
    even_part = jnp.where(lower, 1.0, 0.0)
    odd_part = jnp.where(lower, 0.5, 0.0) + jnp.where(upper, 0.5, 0.0)
    return jnp.where(is_even, even_part, odd_part).astype(jnp.float32)


def ref_kernel(pix, ref_ref, out_ref):
    chunks = pix // IMG

    def build(u, carry):
        off = pl.multiple_of(u * IMG, IMG)
        dst = pl.multiple_of(off + IMG, IMG)
        chunk = ref_ref[:, pl.ds(off, IMG)]
        wide = chunk.astype(jnp.float32)
        out_ref[0, :, pl.ds(dst, IMG)] = pltpu.roll(wide, 1, 1).astype(jnp.bfloat16)
        out_ref[1, :, pl.ds(dst, IMG)] = chunk
        out_ref[2, :, pl.ds(dst, IMG)] = pltpu.roll(wide, IMG - 1, 1).astype(jnp.bfloat16)
        return carry

    lax.fori_loop(0, chunks, build, 0, unroll=8)
    out_ref[:, :, 0:IMG] = out_ref[:, :, pix:pix + IMG]
    out_ref[:, :, pix + IMG:pix + 2 * IMG] = out_ref[:, :, IMG:2 * IMG]


def shifted_refs(templates):
    refcount, pix = templates.shape
    vmem = pl.BlockSpec(memory_space=pltpu.VMEM)
    return pl.pallas_call(
        functools.partial(ref_kernel, pix),
        out_shape=jax.ShapeDtypeStruct((3, refcount, pix + 2 * IMG), jnp.bfloat16),
        in_specs=[vmem],
        out_specs=vmem,
        cost_estimate=pl.CostEstimate(
            flops=0, transcendentals=0, bytes_accessed=templates.size * 8
        ),
    )(templates)


def class_kernel(pix, groups, rows_ref, ref_ref, scale_ref, energy_ref, gain_ref, planes_ref, evid_ref,
                 ext_ref, acc_ref, v_ref):
    chunks = pix // IMG

    def build(u, carry):
        off = pl.multiple_of(u * IMG, IMG)
        dst = pl.multiple_of(off + IMG, IMG)
        chunk = rows_ref[:, pl.ds(off, IMG)]
        wide = chunk.astype(jnp.float32)
        ext_ref[0, :, pl.ds(dst, IMG)] = pltpu.roll(wide, IMG - 1, 1).astype(jnp.bfloat16)
        ext_ref[1, :, pl.ds(dst, IMG)] = chunk
        ext_ref[2, :, pl.ds(dst, IMG)] = pltpu.roll(wide, 1, 1).astype(jnp.bfloat16)
        return carry

    lax.fori_loop(0, chunks, build, 0, unroll=8)
    ext_ref[:, :, 0:IMG] = ext_ref[:, :, pix:pix + IMG]
    ext_ref[:, :, pix + IMG:pix + 2 * IMG] = ext_ref[:, :, IMG:2 * IMG]

    acc_ref[...] = jnp.zeros_like(acc_ref)

    def products(j, carry):
        k0 = pl.multiple_of(j * TK, TK)
        tile = rows_ref[:, pl.ds(k0, TK)]
        for ai, a in enumerate(SHIFTS):
            start = pl.multiple_of(k0 + IMG * (1 + a), IMG)
            for bi in range(3):
                moved = ref_ref[bi, :, pl.ds(start, TK)]
                acc_ref[ai * 3 + bi] += lax.dot_general(
                    moved, tile, (((1,), (1,)), ((), ())), preferred_element_type=jnp.float32
                )
        return carry

    lax.fori_loop(0, pix // TK, products, 0)

    scale = scale_ref[...]
    half_energy = 0.5 * energy_ref[...]
    scores = [scale * (acc_ref[t] - half_energy) for t in range(9)]
    highest = jnp.max(scores[0], axis=0, keepdims=True)
    for t in range(1, 9):
        highest = jnp.maximum(highest, jnp.max(scores[t], axis=0, keepdims=True))
    total = jnp.sum(jnp.exp(scores[0] - highest), axis=0, keepdims=True)
    for t in range(1, 9):
        total = total + jnp.sum(jnp.exp(scores[t] - highest), axis=0, keepdims=True)
    evidence = highest + jnp.log(total)
    evid_ref[...] = evidence
    gain = gain_ref[...]
    gain_hi = gain.astype(jnp.bfloat16)
    gain_lo = (gain - gain_hi.astype(jnp.float32)).astype(jnp.bfloat16)
    depth = gain.shape[0]
    for t in range(9):
        weights = jnp.exp(scores[t] - evidence).astype(jnp.bfloat16)
        mixed = jnp.dot(gain_hi, weights, preferred_element_type=jnp.float32) + jnp.dot(
            gain_lo, weights, preferred_element_type=jnp.float32
        )
        mixed_hi = mixed.astype(jnp.bfloat16).astype(jnp.float32)
        v_ref[t, 0:depth] = mixed_hi
        v_ref[t, depth:2 * depth] = mixed - mixed_hi

    band = pix // groups
    width = band // IMG

    def plane_tiles(j, carry):
        n0 = pl.multiple_of(j * band, band)
        summed = jnp.zeros((2 * depth, band), jnp.float32)
        for ai, a in enumerate(SHIFTS):
            start = pl.multiple_of(n0 + IMG * (1 - a), IMG)
            for bi in range(3):
                summed = summed + jnp.dot(
                    v_ref[ai * 3 + bi].astype(jnp.bfloat16), ext_ref[bi, :, pl.ds(start, band)],
                    preferred_element_type=jnp.float32,
                )
        plane = summed[0:depth] + summed[depth:2 * depth]
        before = lax.rem(j + groups - 1, groups)
        for z in range(depth):
            for u in range(width):
                row = z * (width + 1) + u
                planes_ref[j, pl.ds(row, 1), :] = plane[z:z + 1, u * IMG:(u + 1) * IMG]
            row = z * (width + 1) + width
            planes_ref[before, pl.ds(row, 1), :] = plane[z:z + 1, 0:IMG]
        return carry

    lax.fori_loop(0, groups, plane_tiles, 0)


def class_pass(rows_ext, templates, scale_row, energy_col, gain, pix, groups):
    rowcount = rows_ext.shape[0]
    refcount = templates.shape[1]
    depth = gain.shape[0]
    vmem = pl.BlockSpec(memory_space=pltpu.VMEM)
    flops = 2 * 9 * (refcount + 2 * depth) * rowcount * pix
    cost = pl.CostEstimate(
        flops=flops, transcendentals=10 * refcount * rowcount,
        bytes_accessed=rows_ext.size * 2 + templates.size * 2 + depth * pix * 4,
    )
    return pl.pallas_call(
        functools.partial(class_kernel, pix, groups),
        out_shape=(
            jax.ShapeDtypeStruct((groups, depth * (pix // groups // IMG + 1), IMG), jnp.float32),
            jax.ShapeDtypeStruct((1, rowcount), jnp.float32),
        ),
        in_specs=[vmem] * 5,
        out_specs=(vmem, vmem),
        scratch_shapes=[
            pltpu.VMEM((3, rowcount, pix + 2 * IMG), jnp.bfloat16),
            pltpu.VMEM((9, refcount, rowcount), jnp.float32),
            pltpu.VMEM((9, 2 * depth, rowcount), jnp.float32),
        ],
        compiler_params=pltpu.CompilerParams(vmem_limit_bytes=48 * 1024 * 1024),
        cost_estimate=cost,
    )(rows_ext, templates, scale_row, energy_col, gain)


def on_device(
    particles, particle_precision, particle_class, class_owner, references, insert_weights
):
    sources = lax.axis_size("dev")
    groups = lax.axis_size("grp")
    local_count, pix = particles.shape
    classes = class_owner.shape[0]
    owned_classes = references.shape[0]
    slot_depth = max(2, 2 * local_count // classes)
    labels = particle_class[:, 0]
    catalog = jnp.arange(classes, dtype=jnp.int32)
    position = jnp.sum(
        jnp.where(labels[:, None] == catalog[None, :], class_owner[None, :], 0), axis=1
    )
    ordinal = jnp.arange(local_count, dtype=jnp.int32)
    earlier = (labels[:, None] == labels[None, :]) & (ordinal[None, :] < ordinal[:, None])
    arrival = jnp.sum(earlier, axis=1)
    slot_index = arrival * classes + position
    total_slots = classes * slot_depth
    placing = (jnp.arange(total_slots, dtype=jnp.int32)[:, None] == slot_index[None, :]).astype(
        jnp.bfloat16
    )
    extra = jnp.broadcast_to(particle_precision[:, None], (local_count, IMG))
    carried = jnp.concatenate([particles, extra], axis=1)
    width = pix + IMG
    outgoing = jnp.dot(placing, carried, preferred_element_type=jnp.float32).astype(jnp.bfloat16)
    outgoing = outgoing.reshape(slot_depth, sources, owned_classes * width)
    arrived = lax.all_to_all(outgoing, "dev", split_axis=1, concat_axis=1, tiled=True)
    rows_ext = arrived.reshape(slot_depth * sources, width)
    scale_row = rows_ext[:, pix].astype(jnp.float32).reshape(1, slot_depth * sources)
    templates = references[0]
    energy_col = jnp.sum(jnp.square(templates.astype(jnp.float32)), axis=1).reshape(-1, 1)
    windows, class_evidence = class_pass(
        rows_ext, shifted_refs(templates), scale_row, energy_col, insert_weights, pix, groups
    )
    stacked = class_evidence.reshape(slot_depth, sources)
    returned = lax.all_to_all(stacked, "dev", split_axis=1, concat_axis=1, tiled=True).reshape(
        total_slots
    )
    particle_evidence = jnp.take(returned, slot_index)
    depth = insert_weights.shape[0]
    band = IMG // groups
    here = lax.axis_index("grp")
    mine = lax.dynamic_index_in_dim(windows, here, 0, keepdims=False)
    for step in range(1, groups):
        part = lax.dynamic_index_in_dim(windows, lax.rem(here + step, groups), 0, keepdims=False)
        pairs = [(g, (g + step) % groups) for g in range(groups)]
        mine = mine + lax.ppermute(part, "grp", pairs)
    mine = mine.reshape(depth, band + 1, IMG)
    interp = upsample_table(VOL, IMG)
    across = jnp.einsum("zjv,xv->zjx", mine, interp, precision=lax.Precision.HIGHEST)
    rows_table = local_table(2 * band, band + 1)
    volume = jnp.einsum("yj,zjx->yzx", rows_table, across, precision=lax.Precision.HIGHEST)
    return (volume, particle_evidence)


def solution(mesh):
    placed = (
        P(("grp", "dev"), None),
        P(("grp", "dev")),
        P(("grp", "dev"), None),
        P(),
        P("dev", None, None),
        P("dev", None),
    )
    return jax.shard_map(
        on_device,
        mesh=mesh,
        in_specs=placed,
        out_specs=(P("grp", "dev", None), P(("grp", "dev"))),
        check_vma=False,
    )
```

```python
import functools

import jax
import jax.numpy as jnp
from jax import lax
from jax.experimental import pallas as pl
from jax.experimental.pallas import tpu as pltpu
from jax.sharding import PartitionSpec as P

IMG = 128
VOL = 256
SHIFTS = (-1, 0, 1)
TK = 2048
TN = 1024


def upsample_table(length, source):
    target = jnp.arange(length, dtype=jnp.int32)[:, None]
    anchor = jnp.arange(source, dtype=jnp.int32)[None, :]
    halves = target // 2
    lower = anchor == halves
    upper = anchor == (halves + 1) % source
    is_even = target % 2 == 0
    even_part = jnp.where(lower, 1.0, 0.0)
    odd_part = jnp.where(lower, 0.5, 0.0) + jnp.where(upper, 0.5, 0.0)
    return jnp.where(is_even, even_part, odd_part).astype(jnp.float32)


def local_table(rows, anchors):
    target = jnp.arange(rows, dtype=jnp.int32)[:, None]
    anchor = jnp.arange(anchors, dtype=jnp.int32)[None, :]
    halves = target // 2
    lower = anchor == halves
    upper = anchor == halves + 1
    is_even = target % 2 == 0
    even_part = jnp.where(lower, 1.0, 0.0)
    odd_part = jnp.where(lower, 0.5, 0.0) + jnp.where(upper, 0.5, 0.0)
    return jnp.where(is_even, even_part, odd_part).astype(jnp.float32)


def class_kernel(pix, groups, rows_ref, ref_ref, scale_ref, energy_ref, gain_ref, planes_ref, evid_ref,
                 ext_ref, acc_ref, v_ref):
    chunks = pix // IMG

    def build(u, carry):
        off = pl.multiple_of(u * IMG, IMG)
        dst = pl.multiple_of(off + IMG, IMG)
        chunk = rows_ref[:, pl.ds(off, IMG)]
        wide = chunk.astype(jnp.float32)
        ext_ref[0, :, pl.ds(dst, IMG)] = pltpu.roll(wide, IMG - 1, 1).astype(jnp.bfloat16)
        ext_ref[1, :, pl.ds(dst, IMG)] = chunk
        ext_ref[2, :, pl.ds(dst, IMG)] = pltpu.roll(wide, 1, 1).astype(jnp.bfloat16)
        return carry

    lax.fori_loop(0, chunks, build, 0, unroll=8)
    ext_ref[:, :, 0:IMG] = ext_ref[:, :, pix:pix + IMG]
    ext_ref[:, :, pix + IMG:pix + 2 * IMG] = ext_ref[:, :, IMG:2 * IMG]

    acc_ref[...] = jnp.zeros_like(acc_ref)

    def products(j, carry):
        k0 = pl.multiple_of(j * TK, TK)
        tile = ref_ref[:, pl.ds(k0, TK)]
        for ai, a in enumerate(SHIFTS):
            start = pl.multiple_of(k0 + IMG * (1 - a), IMG)
            for bi in range(3):
                moved = ext_ref[bi, :, pl.ds(start, TK)]
                acc_ref[ai * 3 + bi] += lax.dot_general(
                    tile, moved, (((1,), (1,)), ((), ())), preferred_element_type=jnp.float32
                )
        return carry

    lax.fori_loop(0, pix // TK, products, 0)

    scale = scale_ref[...]
    half_energy = 0.5 * energy_ref[...]
    scores = [scale * (acc_ref[t] - half_energy) for t in range(9)]
    highest = jnp.max(scores[0], axis=0, keepdims=True)
    for t in range(1, 9):
        highest = jnp.maximum(highest, jnp.max(scores[t], axis=0, keepdims=True))
    total = jnp.sum(jnp.exp(scores[0] - highest), axis=0, keepdims=True)
    for t in range(1, 9):
        total = total + jnp.sum(jnp.exp(scores[t] - highest), axis=0, keepdims=True)
    evidence = highest + jnp.log(total)
    evid_ref[...] = evidence
    gain = gain_ref[...]
    gain_hi = gain.astype(jnp.bfloat16)
    gain_lo = (gain - gain_hi.astype(jnp.float32)).astype(jnp.bfloat16)
    depth = gain.shape[0]
    for t in range(9):
        weights = jnp.exp(scores[t] - evidence).astype(jnp.bfloat16)
        mixed = jnp.dot(gain_hi, weights, preferred_element_type=jnp.float32) + jnp.dot(
            gain_lo, weights, preferred_element_type=jnp.float32
        )
        mixed_hi = mixed.astype(jnp.bfloat16).astype(jnp.float32)
        v_ref[t, 0:depth] = mixed_hi
        v_ref[t, depth:2 * depth] = mixed - mixed_hi

    band = pix // groups
    width = band // IMG

    def plane_tiles(j, carry):
        n0 = pl.multiple_of(j * band, band)
        summed = jnp.zeros((2 * depth, band), jnp.float32)
        for ai, a in enumerate(SHIFTS):
            start = pl.multiple_of(n0 + IMG * (1 - a), IMG)
            for bi in range(3):
                summed = summed + jnp.dot(
                    v_ref[ai * 3 + bi].astype(jnp.bfloat16), ext_ref[bi, :, pl.ds(start, band)],
                    preferred_element_type=jnp.float32,
                )
        plane = summed[0:depth] + summed[depth:2 * depth]
        before = lax.rem(j + groups - 1, groups)
        for z in range(depth):
            for u in range(width):
                row = z * (width + 1) + u
                planes_ref[j, pl.ds(row, 1), :] = plane[z:z + 1, u * IMG:(u + 1) * IMG]
            row = z * (width + 1) + width
            planes_ref[before, pl.ds(row, 1), :] = plane[z:z + 1, 0:IMG]
        return carry

    lax.fori_loop(0, groups, plane_tiles, 0)


def class_pass(rows_ext, templates, scale_row, energy_col, gain, pix, groups):
    rowcount = rows_ext.shape[0]
    refcount = templates.shape[0]
    depth = gain.shape[0]
    vmem = pl.BlockSpec(memory_space=pltpu.VMEM)
    flops = 2 * 9 * (refcount + 2 * depth) * rowcount * pix
    cost = pl.CostEstimate(
        flops=flops, transcendentals=10 * refcount * rowcount,
        bytes_accessed=rows_ext.size * 2 + templates.size * 2 + depth * pix * 4,
    )
    return pl.pallas_call(
        functools.partial(class_kernel, pix, groups),
        out_shape=(
            jax.ShapeDtypeStruct((groups, depth * (pix // groups // IMG + 1), IMG), jnp.float32),
            jax.ShapeDtypeStruct((1, rowcount), jnp.float32),
        ),
        in_specs=[vmem] * 5,
        out_specs=(vmem, vmem),
        scratch_shapes=[
            pltpu.VMEM((3, rowcount, pix + 2 * IMG), jnp.bfloat16),
            pltpu.VMEM((9, refcount, rowcount), jnp.float32),
            pltpu.VMEM((9, 2 * depth, rowcount), jnp.float32),
        ],
        compiler_params=pltpu.CompilerParams(vmem_limit_bytes=48 * 1024 * 1024),
        cost_estimate=cost,
    )(rows_ext, templates, scale_row, energy_col, gain)


def on_device(
    particles, particle_precision, particle_class, class_owner, references, insert_weights
):
    sources = lax.axis_size("dev")
    groups = lax.axis_size("grp")
    local_count, pix = particles.shape
    classes = class_owner.shape[0]
    owned_classes = references.shape[0]
    slot_depth = max(2, 2 * local_count // classes)
    labels = particle_class[:, 0]
    catalog = jnp.arange(classes, dtype=jnp.int32)
    position = jnp.sum(
        jnp.where(labels[:, None] == catalog[None, :], class_owner[None, :], 0), axis=1
    )
    ordinal = jnp.arange(local_count, dtype=jnp.int32)
    earlier = (labels[:, None] == labels[None, :]) & (ordinal[None, :] < ordinal[:, None])
    arrival = jnp.sum(earlier, axis=1)
    slot_index = arrival * classes + position
    total_slots = classes * slot_depth
    placing = (jnp.arange(total_slots, dtype=jnp.int32)[:, None] == slot_index[None, :]).astype(
        jnp.bfloat16
    )
    extra = jnp.broadcast_to(particle_precision[:, None], (local_count, IMG))
    carried = jnp.concatenate([particles, extra], axis=1)
    width = pix + IMG
    outgoing = jnp.dot(placing, carried, preferred_element_type=jnp.float32).astype(jnp.bfloat16)
    outgoing = outgoing.reshape(slot_depth, sources, owned_classes * width)
    arrived = lax.all_to_all(outgoing, "dev", split_axis=1, concat_axis=1, tiled=True)
    rows_ext = arrived.reshape(slot_depth * sources, width)
    scale_row = rows_ext[:, pix].astype(jnp.float32).reshape(1, slot_depth * sources)
    templates = references[0]
    energy_col = jnp.sum(jnp.square(templates.astype(jnp.float32)), axis=1).reshape(-1, 1)
    windows, class_evidence = class_pass(
        rows_ext, templates, scale_row, energy_col, insert_weights, pix, groups
    )
    stacked = class_evidence.reshape(slot_depth, sources)
    returned = lax.all_to_all(stacked, "dev", split_axis=1, concat_axis=1, tiled=True).reshape(
        total_slots
    )
    particle_evidence = jnp.take(returned, slot_index)
    depth = insert_weights.shape[0]
    band = IMG // groups
    here = lax.axis_index("grp")
    mine = lax.dynamic_index_in_dim(windows, here, 0, keepdims=False)
    for step in range(1, groups):
        part = lax.dynamic_index_in_dim(windows, lax.rem(here + step, groups), 0, keepdims=False)
        pairs = [(g, (g + step) % groups) for g in range(groups)]
        mine = mine + lax.ppermute(part, "grp", pairs)
    interp = upsample_table(VOL, IMG)
    across = jnp.dot(mine, interp.T, precision=lax.Precision.HIGHEST)
    rows_table = local_table(2 * band, band + 1)
    eye = jnp.eye(depth, dtype=jnp.float32)
    block = (rows_table[:, None, None, :] * eye[None, :, :, None]).reshape(
        2 * band * depth, depth * (band + 1)
    )
    volume = jnp.dot(block, across, precision=lax.Precision.HIGHEST).reshape(2 * band, depth, VOL)
    return (volume, particle_evidence)


def solution(mesh):
    placed = (
        P(("grp", "dev"), None),
        P(("grp", "dev")),
        P(("grp", "dev"), None),
        P(),
        P("dev", None, None),
        P("dev", None),
    )
    return jax.shard_map(
        on_device,
        mesh=mesh,
        in_specs=placed,
        out_specs=(P("grp", "dev", None), P(("grp", "dev"))),
        check_vma=False,
    )
```

```python
import functools

import jax
import jax.numpy as jnp
from jax import lax
from jax.experimental import pallas as pl
from jax.experimental.pallas import tpu as pltpu
from jax.sharding import PartitionSpec as P

IMG = 128
VOL = 256
SHIFTS = (-1, 0, 1)
TK = 8192
TN = 1024


def upsample_table(length, source):
    target = jnp.arange(length, dtype=jnp.int32)[:, None]
    anchor = jnp.arange(source, dtype=jnp.int32)[None, :]
    halves = target // 2
    lower = anchor == halves
    upper = anchor == (halves + 1) % source
    is_even = target % 2 == 0
    even_part = jnp.where(lower, 1.0, 0.0)
    odd_part = jnp.where(lower, 0.5, 0.0) + jnp.where(upper, 0.5, 0.0)
    return jnp.where(is_even, even_part, odd_part).astype(jnp.float32)


def local_table(rows, anchors):
    target = jnp.arange(rows, dtype=jnp.int32)[:, None]
    anchor = jnp.arange(anchors, dtype=jnp.int32)[None, :]
    halves = target // 2
    lower = anchor == halves
    upper = anchor == halves + 1
    is_even = target % 2 == 0
    even_part = jnp.where(lower, 1.0, 0.0)
    odd_part = jnp.where(lower, 0.5, 0.0) + jnp.where(upper, 0.5, 0.0)
    return jnp.where(is_even, even_part, odd_part).astype(jnp.float32)


def class_kernel(pix, groups, rows_ref, ref_ref, scale_ref, energy_ref, gain_ref, planes_ref, evid_ref,
                 ext_ref, acc_ref, v_ref):
    chunks = pix // IMG

    def build(u, carry):
        off = pl.multiple_of(u * IMG, IMG)
        dst = pl.multiple_of(off + IMG, IMG)
        chunk = rows_ref[:, pl.ds(off, IMG)]
        wide = chunk.astype(jnp.float32)
        ext_ref[0, :, pl.ds(dst, IMG)] = pltpu.roll(wide, IMG - 1, 1).astype(jnp.bfloat16)
        ext_ref[1, :, pl.ds(dst, IMG)] = chunk
        ext_ref[2, :, pl.ds(dst, IMG)] = pltpu.roll(wide, 1, 1).astype(jnp.bfloat16)
        return carry

    lax.fori_loop(0, chunks, build, 0, unroll=32)
    ext_ref[:, :, 0:IMG] = ext_ref[:, :, pix:pix + IMG]
    ext_ref[:, :, pix + IMG:pix + 2 * IMG] = ext_ref[:, :, IMG:2 * IMG]

    acc_ref[...] = jnp.zeros_like(acc_ref)

    def products(j, carry):
        k0 = pl.multiple_of(j * TK, TK)
        tile = ref_ref[:, pl.ds(k0, TK)]
        for ai, a in enumerate(SHIFTS):
            start = pl.multiple_of(k0 + IMG * (1 - a), IMG)
            for bi in range(3):
                moved = ext_ref[bi, :, pl.ds(start, TK)]
                acc_ref[ai * 3 + bi] += lax.dot_general(
                    tile, moved, (((1,), (1,)), ((), ())), preferred_element_type=jnp.float32
                )
        return carry

    lax.fori_loop(0, pix // TK, products, 0)

    scale = scale_ref[...]
    half_energy = 0.5 * energy_ref[...]
    scores = [scale * (acc_ref[t] - half_energy) for t in range(9)]
    highest = jnp.max(scores[0], axis=0, keepdims=True)
    for t in range(1, 9):
        highest = jnp.maximum(highest, jnp.max(scores[t], axis=0, keepdims=True))
    total = jnp.sum(jnp.exp(scores[0] - highest), axis=0, keepdims=True)
    for t in range(1, 9):
        total = total + jnp.sum(jnp.exp(scores[t] - highest), axis=0, keepdims=True)
    evidence = highest + jnp.log(total)
    evid_ref[...] = evidence
    gain = gain_ref[...]
    gain_hi = gain.astype(jnp.bfloat16)
    gain_lo = (gain - gain_hi.astype(jnp.float32)).astype(jnp.bfloat16)
    depth = gain.shape[0]
    for t in range(9):
        weights = jnp.exp(scores[t] - evidence).astype(jnp.bfloat16)
        mixed = jnp.dot(gain_hi, weights, preferred_element_type=jnp.float32) + jnp.dot(
            gain_lo, weights, preferred_element_type=jnp.float32
        )
        mixed_hi = mixed.astype(jnp.bfloat16).astype(jnp.float32)
        v_ref[t, 0:depth] = mixed_hi
        v_ref[t, depth:2 * depth] = mixed - mixed_hi

    band = pix // groups
    width = band // IMG

    def plane_tiles(j, carry):
        n0 = pl.multiple_of(j * band, band)
        summed = jnp.zeros((2 * depth, band), jnp.float32)
        for ai, a in enumerate(SHIFTS):
            start = pl.multiple_of(n0 + IMG * (1 - a), IMG)
            for bi in range(3):
                summed = summed + jnp.dot(
                    v_ref[ai * 3 + bi].astype(jnp.bfloat16), ext_ref[bi, :, pl.ds(start, band)],
                    preferred_element_type=jnp.float32,
                )
        plane = summed[0:depth] + summed[depth:2 * depth]
        before = lax.rem(j + groups - 1, groups)
        for z in range(depth):
            for u in range(width):
                row = z * (width + 1) + u
                planes_ref[j, pl.ds(row, 1), :] = plane[z:z + 1, u * IMG:(u + 1) * IMG]
            row = z * (width + 1) + width
            planes_ref[before, pl.ds(row, 1), :] = plane[z:z + 1, 0:IMG]
        return carry

    lax.fori_loop(0, groups, plane_tiles, 0)


def class_pass(rows_ext, templates, scale_row, energy_col, gain, pix, groups):
    rowcount = rows_ext.shape[0]
    refcount = templates.shape[0]
    depth = gain.shape[0]
    vmem = pl.BlockSpec(memory_space=pltpu.VMEM)
    flops = 2 * 9 * (refcount + 2 * depth) * rowcount * pix
    cost = pl.CostEstimate(
        flops=flops, transcendentals=10 * refcount * rowcount,
        bytes_accessed=rows_ext.size * 2 + templates.size * 2 + depth * pix * 4,
    )
    return pl.pallas_call(
        functools.partial(class_kernel, pix, groups),
        out_shape=(
            jax.ShapeDtypeStruct((groups, depth * (pix // groups // IMG + 1), IMG), jnp.float32),
            jax.ShapeDtypeStruct((1, rowcount), jnp.float32),
        ),
        in_specs=[vmem] * 5,
        out_specs=(vmem, vmem),
        scratch_shapes=[
            pltpu.VMEM((3, rowcount, pix + 2 * IMG), jnp.bfloat16),
            pltpu.VMEM((9, refcount, rowcount), jnp.float32),
            pltpu.VMEM((9, 2 * depth, rowcount), jnp.float32),
        ],
        compiler_params=pltpu.CompilerParams(vmem_limit_bytes=48 * 1024 * 1024),
        cost_estimate=cost,
    )(rows_ext, templates, scale_row, energy_col, gain)


def on_device(
    particles, particle_precision, particle_class, class_owner, references, insert_weights
):
    sources = lax.axis_size("dev")
    groups = lax.axis_size("grp")
    local_count, pix = particles.shape
    classes = class_owner.shape[0]
    owned_classes = references.shape[0]
    slot_depth = max(2, 2 * local_count // classes)
    labels = particle_class[:, 0]
    catalog = jnp.arange(classes, dtype=jnp.int32)
    position = jnp.sum(
        jnp.where(labels[:, None] == catalog[None, :], class_owner[None, :], 0), axis=1
    )
    ordinal = jnp.arange(local_count, dtype=jnp.int32)
    earlier = (labels[:, None] == labels[None, :]) & (ordinal[None, :] < ordinal[:, None])
    arrival = jnp.sum(earlier, axis=1)
    slot_index = arrival * classes + position
    total_slots = classes * slot_depth
    placing = (jnp.arange(total_slots, dtype=jnp.int32)[:, None] == slot_index[None, :]).astype(
        jnp.bfloat16
    )
    extra = jnp.broadcast_to(particle_precision[:, None], (local_count, IMG))
    carried = jnp.concatenate([particles, extra], axis=1)
    width = pix + IMG
    outgoing = jnp.dot(placing, carried, preferred_element_type=jnp.float32).astype(jnp.bfloat16)
    outgoing = outgoing.reshape(slot_depth, sources, owned_classes * width)
    arrived = lax.all_to_all(outgoing, "dev", split_axis=1, concat_axis=1, tiled=True)
    rows_ext = arrived.reshape(slot_depth * sources, width)
    scale_row = rows_ext[:, pix].astype(jnp.float32).reshape(1, slot_depth * sources)
    templates = references[0]
    energy_col = jnp.sum(jnp.square(templates.astype(jnp.float32)), axis=1).reshape(-1, 1)
    windows, class_evidence = class_pass(
        rows_ext, templates, scale_row, energy_col, insert_weights, pix, groups
    )
    stacked = class_evidence.reshape(slot_depth, sources)
    returned = lax.all_to_all(stacked, "dev", split_axis=1, concat_axis=1, tiled=True).reshape(
        total_slots
    )
    particle_evidence = jnp.take(returned, slot_index)
    depth = insert_weights.shape[0]
    band = IMG // groups
    here = lax.axis_index("grp")
    mine = lax.dynamic_index_in_dim(windows, here, 0, keepdims=False)
    for step in range(1, groups):
        part = lax.dynamic_index_in_dim(windows, lax.rem(here + step, groups), 0, keepdims=False)
        pairs = [(g, (g + step) % groups) for g in range(groups)]
        mine = mine + lax.ppermute(part, "grp", pairs)
    interp = upsample_table(VOL, IMG)
    across = jnp.dot(mine, interp.T, precision=lax.Precision.HIGHEST)
    rows_table = local_table(2 * band, band + 1)
    eye = jnp.eye(depth, dtype=jnp.float32)
    block = (rows_table[:, None, None, :] * eye[None, :, :, None]).reshape(
        2 * band * depth, depth * (band + 1)
    )
    volume = jnp.dot(block, across, precision=lax.Precision.HIGHEST).reshape(2 * band, depth, VOL)
    return (volume, particle_evidence)


def solution(mesh):
    placed = (
        P(("grp", "dev"), None),
        P(("grp", "dev")),
        P(("grp", "dev"), None),
        P(),
        P("dev", None, None),
        P("dev", None),
    )
    return jax.shard_map(
        on_device,
        mesh=mesh,
        in_specs=placed,
        out_specs=(P("grp", "dev", None), P(("grp", "dev"))),
        check_vma=False,
    )
```

```python
import functools

import jax
import jax.numpy as jnp
from jax import lax
from jax.experimental import pallas as pl
from jax.experimental.pallas import tpu as pltpu
from jax.sharding import PartitionSpec as P

IMG = 128
VOL = 256
SHIFTS = (-1, 0, 1)
TK = 16384
TN = 1024


def upsample_table(length, source):
    target = jnp.arange(length, dtype=jnp.int32)[:, None]
    anchor = jnp.arange(source, dtype=jnp.int32)[None, :]
    halves = target // 2
    lower = anchor == halves
    upper = anchor == (halves + 1) % source
    is_even = target % 2 == 0
    even_part = jnp.where(lower, 1.0, 0.0)
    odd_part = jnp.where(lower, 0.5, 0.0) + jnp.where(upper, 0.5, 0.0)
    return jnp.where(is_even, even_part, odd_part).astype(jnp.float32)


def local_table(rows, anchors):
    target = jnp.arange(rows, dtype=jnp.int32)[:, None]
    anchor = jnp.arange(anchors, dtype=jnp.int32)[None, :]
    halves = target // 2
    lower = anchor == halves
    upper = anchor == halves + 1
    is_even = target % 2 == 0
    even_part = jnp.where(lower, 1.0, 0.0)
    odd_part = jnp.where(lower, 0.5, 0.0) + jnp.where(upper, 0.5, 0.0)
    return jnp.where(is_even, even_part, odd_part).astype(jnp.float32)


def class_kernel(pix, groups, rows_ref, ref_ref, scale_ref, energy_ref, gain_ref, planes_ref, evid_ref,
                 ext_ref, acc_ref, v_ref):
    chunks = pix // IMG

    def build(u, carry):
        off = pl.multiple_of(u * IMG, IMG)
        dst = pl.multiple_of(off + IMG, IMG)
        chunk = rows_ref[:, pl.ds(off, IMG)]
        wide = chunk.astype(jnp.float32)
        ext_ref[0, :, pl.ds(dst, IMG)] = pltpu.roll(wide, IMG - 1, 1).astype(jnp.bfloat16)
        ext_ref[1, :, pl.ds(dst, IMG)] = chunk
        ext_ref[2, :, pl.ds(dst, IMG)] = pltpu.roll(wide, 1, 1).astype(jnp.bfloat16)
        return carry

    lax.fori_loop(0, chunks, build, 0, unroll=32)
    ext_ref[:, :, 0:IMG] = ext_ref[:, :, pix:pix + IMG]
    ext_ref[:, :, pix + IMG:pix + 2 * IMG] = ext_ref[:, :, IMG:2 * IMG]

    acc_ref[...] = jnp.zeros_like(acc_ref)

    def products(j, carry):
        k0 = pl.multiple_of(j * TK, TK)
        tile = ref_ref[:, pl.ds(k0, TK)]
        for ai, a in enumerate(SHIFTS):
            start = pl.multiple_of(k0 + IMG * (1 - a), IMG)
            for bi in range(3):
                moved = ext_ref[bi, :, pl.ds(start, TK)]
                acc_ref[ai * 3 + bi] += lax.dot_general(
                    tile, moved, (((1,), (1,)), ((), ())), preferred_element_type=jnp.float32
                )
        return carry

    lax.fori_loop(0, pix // TK, products, 0)

    scale = scale_ref[...]
    half_energy = 0.5 * energy_ref[...]
    scores = [scale * (acc_ref[t] - half_energy) for t in range(9)]
    highest = jnp.max(scores[0], axis=0, keepdims=True)
    for t in range(1, 9):
        highest = jnp.maximum(highest, jnp.max(scores[t], axis=0, keepdims=True))
    total = jnp.sum(jnp.exp(scores[0] - highest), axis=0, keepdims=True)
    for t in range(1, 9):
        total = total + jnp.sum(jnp.exp(scores[t] - highest), axis=0, keepdims=True)
    evidence = highest + jnp.log(total)
    evid_ref[...] = evidence
    gain = gain_ref[...]
    gain_hi = gain.astype(jnp.bfloat16)
    gain_lo = (gain - gain_hi.astype(jnp.float32)).astype(jnp.bfloat16)
    depth = gain.shape[0]
    for t in range(9):
        weights = jnp.exp(scores[t] - evidence).astype(jnp.bfloat16)
        mixed = jnp.dot(gain_hi, weights, preferred_element_type=jnp.float32) + jnp.dot(
            gain_lo, weights, preferred_element_type=jnp.float32
        )
        mixed_hi = mixed.astype(jnp.bfloat16).astype(jnp.float32)
        v_ref[t, 0:depth] = mixed_hi
        v_ref[t, depth:2 * depth] = mixed - mixed_hi

    band = pix // groups
    width = band // IMG

    def plane_tiles(jj, carry):
        n0 = pl.multiple_of(jj * 2 * band, 2 * band)
        summed = jnp.zeros((2 * depth, 2 * band), jnp.float32)
        for ai, a in enumerate(SHIFTS):
            start = pl.multiple_of(n0 + IMG * (1 - a), IMG)
            for bi in range(3):
                summed = summed + jnp.dot(
                    v_ref[ai * 3 + bi].astype(jnp.bfloat16), ext_ref[bi, :, pl.ds(start, 2 * band)],
                    preferred_element_type=jnp.float32,
                )
        both = summed[0:depth] + summed[depth:2 * depth]
        for half in range(2):
            j = jj * 2 + half
            plane = both[:, half * band:(half + 1) * band]
            before = lax.rem(j + groups - 1, groups)
            for z in range(depth):
                for u in range(width):
                    row = z * (width + 1) + u
                    planes_ref[j, pl.ds(row, 1), :] = plane[z:z + 1, u * IMG:(u + 1) * IMG]
                row = z * (width + 1) + width
                planes_ref[before, pl.ds(row, 1), :] = plane[z:z + 1, 0:IMG]
        return carry

    lax.fori_loop(0, groups // 2, plane_tiles, 0)


def class_pass(rows_ext, templates, scale_row, energy_col, gain, pix, groups):
    rowcount = rows_ext.shape[0]
    refcount = templates.shape[0]
    depth = gain.shape[0]
    vmem = pl.BlockSpec(memory_space=pltpu.VMEM)
    flops = 2 * 9 * (refcount + 2 * depth) * rowcount * pix
    cost = pl.CostEstimate(
        flops=flops, transcendentals=10 * refcount * rowcount,
        bytes_accessed=rows_ext.size * 2 + templates.size * 2 + depth * pix * 4,
    )
    return pl.pallas_call(
        functools.partial(class_kernel, pix, groups),
        out_shape=(
            jax.ShapeDtypeStruct((groups, depth * (pix // groups // IMG + 1), IMG), jnp.float32),
            jax.ShapeDtypeStruct((1, rowcount), jnp.float32),
        ),
        in_specs=[vmem] * 5,
        out_specs=(vmem, vmem),
        scratch_shapes=[
            pltpu.VMEM((3, rowcount, pix + 2 * IMG), jnp.bfloat16),
            pltpu.VMEM((9, refcount, rowcount), jnp.float32),
            pltpu.VMEM((9, 2 * depth, rowcount), jnp.float32),
        ],
        compiler_params=pltpu.CompilerParams(vmem_limit_bytes=48 * 1024 * 1024),
        cost_estimate=cost,
    )(rows_ext, templates, scale_row, energy_col, gain)


def on_device(
    particles, particle_precision, particle_class, class_owner, references, insert_weights
):
    sources = lax.axis_size("dev")
    groups = lax.axis_size("grp")
    local_count, pix = particles.shape
    classes = class_owner.shape[0]
    owned_classes = references.shape[0]
    slot_depth = max(2, 2 * local_count // classes)
    labels = particle_class[:, 0]
    catalog = jnp.arange(classes, dtype=jnp.int32)
    position = jnp.sum(
        jnp.where(labels[:, None] == catalog[None, :], class_owner[None, :], 0), axis=1
    )
    ordinal = jnp.arange(local_count, dtype=jnp.int32)
    earlier = (labels[:, None] == labels[None, :]) & (ordinal[None, :] < ordinal[:, None])
    arrival = jnp.sum(earlier, axis=1)
    slot_index = arrival * classes + position
    total_slots = classes * slot_depth
    placing = (jnp.arange(total_slots, dtype=jnp.int32)[:, None] == slot_index[None, :]).astype(
        jnp.bfloat16
    )
    extra = jnp.broadcast_to(particle_precision[:, None], (local_count, IMG))
    carried = jnp.concatenate([particles, extra], axis=1)
    width = pix + IMG
    outgoing = jnp.dot(placing, carried, preferred_element_type=jnp.float32).astype(jnp.bfloat16)
    outgoing = outgoing.reshape(slot_depth, sources, owned_classes * width)
    arrived = lax.all_to_all(outgoing, "dev", split_axis=1, concat_axis=1, tiled=True)
    rows_ext = arrived.reshape(slot_depth * sources, width)
    scale_row = rows_ext[:, pix].astype(jnp.float32).reshape(1, slot_depth * sources)
    templates = references[0]
    energy_col = jnp.sum(jnp.square(templates.astype(jnp.float32)), axis=1).reshape(-1, 1)
    windows, class_evidence = class_pass(
        rows_ext, templates, scale_row, energy_col, insert_weights, pix, groups
    )
    stacked = class_evidence.reshape(slot_depth, sources)
    returned = lax.all_to_all(stacked, "dev", split_axis=1, concat_axis=1, tiled=True).reshape(
        total_slots
    )
    particle_evidence = jnp.take(returned, slot_index)
    depth = insert_weights.shape[0]
    band = IMG // groups
    here = lax.axis_index("grp")
    mine = lax.dynamic_index_in_dim(windows, here, 0, keepdims=False)
    for step in range(1, groups):
        part = lax.dynamic_index_in_dim(windows, lax.rem(here + step, groups), 0, keepdims=False)
        pairs = [(g, (g + step) % groups) for g in range(groups)]
        mine = mine + lax.ppermute(part, "grp", pairs)
    interp = upsample_table(VOL, IMG)
    across = jnp.dot(mine, interp.T, precision=lax.Precision.HIGHEST)
    rows_table = local_table(2 * band, band + 1)
    eye = jnp.eye(depth, dtype=jnp.float32)
    block = (rows_table[:, None, None, :] * eye[None, :, :, None]).reshape(
        2 * band * depth, depth * (band + 1)
    )
    volume = jnp.dot(block, across, precision=lax.Precision.HIGHEST).reshape(2 * band, depth, VOL)
    return (volume, particle_evidence)


def solution(mesh):
    placed = (
        P(("grp", "dev"), None),
        P(("grp", "dev")),
        P(("grp", "dev"), None),
        P(),
        P("dev", None, None),
        P("dev", None),
    )
    return jax.shard_map(
        on_device,
        mesh=mesh,
        in_specs=placed,
        out_specs=(P("grp", "dev", None), P(("grp", "dev"))),
        check_vma=False,
    )
```

```python
import functools

import jax
import jax.numpy as jnp
from jax import lax
from jax.experimental import pallas as pl
from jax.experimental.pallas import tpu as pltpu
from jax.sharding import PartitionSpec as P

IMG = 128
VOL = 256
SHIFTS = (-1, 0, 1)
TK = 16384
TN = 1024


def upsample_table(length, source):
    target = jnp.arange(length, dtype=jnp.int32)[:, None]
    anchor = jnp.arange(source, dtype=jnp.int32)[None, :]
    halves = target // 2
    lower = anchor == halves
    upper = anchor == (halves + 1) % source
    is_even = target % 2 == 0
    even_part = jnp.where(lower, 1.0, 0.0)
    odd_part = jnp.where(lower, 0.5, 0.0) + jnp.where(upper, 0.5, 0.0)
    return jnp.where(is_even, even_part, odd_part).astype(jnp.float32)


def local_table(rows, anchors):
    target = jnp.arange(rows, dtype=jnp.int32)[:, None]
    anchor = jnp.arange(anchors, dtype=jnp.int32)[None, :]
    halves = target // 2
    lower = anchor == halves
    upper = anchor == halves + 1
    is_even = target % 2 == 0
    even_part = jnp.where(lower, 1.0, 0.0)
    odd_part = jnp.where(lower, 0.5, 0.0) + jnp.where(upper, 0.5, 0.0)
    return jnp.where(is_even, even_part, odd_part).astype(jnp.float32)


def class_kernel(pix, groups, rows_ref, ref_ref, scale_ref, energy_ref, gain_ref, planes_ref, evid_ref,
                 ext_ref, acc_ref, v_ref):
    chunks = pix // IMG

    def build(u, carry):
        off = pl.multiple_of(u * IMG, IMG)
        dst = pl.multiple_of(off + IMG, IMG)
        chunk = rows_ref[:, pl.ds(off, IMG)]
        wide = chunk.astype(jnp.float32)
        ext_ref[0, :, pl.ds(dst, IMG)] = pltpu.roll(wide, IMG - 1, 1).astype(jnp.bfloat16)
        ext_ref[1, :, pl.ds(dst, IMG)] = chunk
        ext_ref[2, :, pl.ds(dst, IMG)] = pltpu.roll(wide, 1, 1).astype(jnp.bfloat16)
        return carry

    lax.fori_loop(0, chunks, build, 0, unroll=32)
    ext_ref[:, :, 0:IMG] = ext_ref[:, :, pix:pix + IMG]
    ext_ref[:, :, pix + IMG:pix + 2 * IMG] = ext_ref[:, :, IMG:2 * IMG]

    acc_ref[...] = jnp.zeros_like(acc_ref)

    def products(j, carry):
        k0 = pl.multiple_of(j * TK, TK)
        tile = ref_ref[:, pl.ds(k0, TK)]
        for ai, a in enumerate(SHIFTS):
            start = pl.multiple_of(k0 + IMG * (1 - a), IMG)
            for bi in range(3):
                moved = ext_ref[bi, :, pl.ds(start, TK)]
                acc_ref[ai * 3 + bi] += lax.dot_general(
                    tile, moved, (((1,), (1,)), ((), ())), preferred_element_type=jnp.float32
                )
        return carry

    lax.fori_loop(0, pix // TK, products, 0)

    scale = scale_ref[...]
    half_energy = 0.5 * energy_ref[...]
    scores = [scale * (acc_ref[t] - half_energy) for t in range(9)]
    highest = jnp.max(scores[0], axis=0, keepdims=True)
    for t in range(1, 9):
        highest = jnp.maximum(highest, jnp.max(scores[t], axis=0, keepdims=True))
    total = jnp.sum(jnp.exp(scores[0] - highest), axis=0, keepdims=True)
    for t in range(1, 9):
        total = total + jnp.sum(jnp.exp(scores[t] - highest), axis=0, keepdims=True)
    evidence = highest + jnp.log(total)
    evid_ref[...] = evidence
    gain = gain_ref[...]
    gain_hi = gain.astype(jnp.bfloat16)
    gain_lo = (gain - gain_hi.astype(jnp.float32)).astype(jnp.bfloat16)
    depth = gain.shape[0]
    for t in range(9):
        weights = jnp.exp(scores[t] - evidence).astype(jnp.bfloat16)
        mixed = jnp.dot(gain_hi, weights, preferred_element_type=jnp.float32) + jnp.dot(
            gain_lo, weights, preferred_element_type=jnp.float32
        )
        mixed_hi = mixed.astype(jnp.bfloat16).astype(jnp.float32)
        v_ref[t, 0:depth] = mixed_hi
        v_ref[t, depth:2 * depth] = mixed - mixed_hi

    band = pix // groups
    width = band // IMG

    def plane_tiles(jj, carry):
        n0 = pl.multiple_of(jj * 2 * band, 2 * band)
        summed = jnp.zeros((2 * depth, 2 * band), jnp.float32)
        for ai, a in enumerate(SHIFTS):
            start = pl.multiple_of(n0 + IMG * (1 - a), IMG)
            for bi in range(3):
                summed = summed + jnp.dot(
                    v_ref[ai * 3 + bi].astype(jnp.bfloat16), ext_ref[bi, :, pl.ds(start, 2 * band)],
                    preferred_element_type=jnp.float32,
                )
        both = summed[0:depth] + summed[depth:2 * depth]
        for half in range(2):
            j = jj * 2 + half
            plane = both[:, half * band:(half + 1) * band]
            before = lax.rem(j + groups - 1, groups)
            for z in range(depth):
                for u in range(width):
                    row = z * (width + 1) + u
                    planes_ref[j, pl.ds(row, 1), :] = plane[z:z + 1, u * IMG:(u + 1) * IMG]
                row = z * (width + 1) + width
                planes_ref[before, pl.ds(row, 1), :] = plane[z:z + 1, 0:IMG]
        return carry

    lax.fori_loop(0, groups // 2, plane_tiles, 0)


def class_pass(rows_ext, templates, scale_row, energy_col, gain, pix, groups):
    rowcount = rows_ext.shape[0]
    refcount = templates.shape[0]
    depth = gain.shape[0]
    vmem = pl.BlockSpec(memory_space=pltpu.VMEM)
    flops = 2 * 9 * (refcount + 2 * depth) * rowcount * pix
    cost = pl.CostEstimate(
        flops=flops, transcendentals=10 * refcount * rowcount,
        bytes_accessed=rows_ext.size * 2 + templates.size * 2 + depth * pix * 4,
    )
    return pl.pallas_call(
        functools.partial(class_kernel, pix, groups),
        out_shape=(
            jax.ShapeDtypeStruct((groups, depth * (pix // groups // IMG + 1), IMG), jnp.float32),
            jax.ShapeDtypeStruct((1, rowcount), jnp.float32),
        ),
        in_specs=[vmem] * 5,
        out_specs=(vmem, vmem),
        scratch_shapes=[
            pltpu.VMEM((3, rowcount, pix + 2 * IMG), jnp.bfloat16),
            pltpu.VMEM((9, refcount, rowcount), jnp.float32),
            pltpu.VMEM((9, 2 * depth, rowcount), jnp.float32),
        ],
        compiler_params=pltpu.CompilerParams(vmem_limit_bytes=48 * 1024 * 1024),
        cost_estimate=cost,
    )(rows_ext, templates, scale_row, energy_col, gain)


def on_device(
    particles, particle_precision, particle_class, class_owner, references, insert_weights
):
    sources = lax.axis_size("dev")
    groups = lax.axis_size("grp")
    local_count, pix = particles.shape
    classes = class_owner.shape[0]
    owned_classes = references.shape[0]
    slot_depth = max(2, 2 * local_count // classes)
    labels = particle_class[:, 0]
    catalog = jnp.arange(classes, dtype=jnp.int32)
    position = jnp.sum(
        jnp.where(labels[:, None] == catalog[None, :], class_owner[None, :], 0), axis=1
    )
    ordinal = jnp.arange(local_count, dtype=jnp.int32)
    earlier = (labels[:, None] == labels[None, :]) & (ordinal[None, :] < ordinal[:, None])
    arrival = jnp.sum(earlier, axis=1)
    slot_index = arrival * classes + position
    total_slots = classes * slot_depth
    placing = (jnp.arange(total_slots, dtype=jnp.int32)[:, None] == slot_index[None, :]).astype(
        jnp.bfloat16
    )
    extra = jnp.broadcast_to(particle_precision[:, None], (local_count, IMG))
    carried = jnp.concatenate([particles, extra], axis=1)
    width = pix + IMG
    outgoing = jnp.dot(placing, carried, preferred_element_type=jnp.float32).astype(jnp.bfloat16)
    outgoing = outgoing.reshape(slot_depth, sources, owned_classes * width)
    arrived = lax.all_to_all(outgoing, "dev", split_axis=1, concat_axis=1, tiled=True)
    rows_ext = arrived.reshape(slot_depth * sources, width)
    scale_row = rows_ext[:, pix].astype(jnp.float32).reshape(1, slot_depth * sources)
    templates = references[0]
    energy_col = jnp.sum(jnp.square(templates.astype(jnp.float32)), axis=1).reshape(-1, 1)
    windows, class_evidence = class_pass(
        rows_ext, templates, scale_row, energy_col, insert_weights, pix, groups
    )
    stacked = class_evidence.reshape(slot_depth, sources)
    returned = lax.all_to_all(stacked, "dev", split_axis=1, concat_axis=1, tiled=True).reshape(
        total_slots
    )
    particle_evidence = jnp.take(returned, slot_index)
    depth = insert_weights.shape[0]
    band = IMG // groups
    here = lax.axis_index("grp")
    mine = lax.dynamic_index_in_dim(windows, here, 0, keepdims=False)
    for step in range(1, groups):
        part = lax.dynamic_index_in_dim(windows, lax.rem(here + step, groups), 0, keepdims=False)
        pairs = [(g, (g + step) % groups) for g in range(groups)]
        mine = mine + lax.ppermute(part, "grp", pairs)
    interp = upsample_table(VOL, IMG)
    across = jnp.dot(mine, interp.T, precision=lax.Precision.HIGH)
    rows_table = local_table(2 * band, band + 1)
    eye = jnp.eye(depth, dtype=jnp.float32)
    block = (rows_table[:, None, None, :] * eye[None, :, :, None]).reshape(
        2 * band * depth, depth * (band + 1)
    )
    volume = jnp.dot(block, across, precision=lax.Precision.HIGH).reshape(2 * band, depth, VOL)
    return (volume, particle_evidence)


def solution(mesh):
    placed = (
        P(("grp", "dev"), None),
        P(("grp", "dev")),
        P(("grp", "dev"), None),
        P(),
        P("dev", None, None),
        P("dev", None),
    )
    return jax.shard_map(
        on_device,
        mesh=mesh,
        in_specs=placed,
        out_specs=(P("grp", "dev", None), P(("grp", "dev"))),
        check_vma=False,
    )
```

```python
import functools

import jax
import jax.numpy as jnp
from jax import lax
from jax.experimental import pallas as pl
from jax.experimental.pallas import tpu as pltpu
from jax.sharding import PartitionSpec as P

IMG = 128
VOL = 256
SHIFTS = (-1, 0, 1)
TK = 16384
TN = 1024


def upsample_table(length, source):
    target = jnp.arange(length, dtype=jnp.int32)[:, None]
    anchor = jnp.arange(source, dtype=jnp.int32)[None, :]
    halves = target // 2
    lower = anchor == halves
    upper = anchor == (halves + 1) % source
    is_even = target % 2 == 0
    even_part = jnp.where(lower, 1.0, 0.0)
    odd_part = jnp.where(lower, 0.5, 0.0) + jnp.where(upper, 0.5, 0.0)
    return jnp.where(is_even, even_part, odd_part).astype(jnp.float32)


def local_table(rows, anchors):
    target = jnp.arange(rows, dtype=jnp.int32)[:, None]
    anchor = jnp.arange(anchors, dtype=jnp.int32)[None, :]
    halves = target // 2
    lower = anchor == halves
    upper = anchor == halves + 1
    is_even = target % 2 == 0
    even_part = jnp.where(lower, 1.0, 0.0)
    odd_part = jnp.where(lower, 0.5, 0.0) + jnp.where(upper, 0.5, 0.0)
    return jnp.where(is_even, even_part, odd_part).astype(jnp.float32)


def class_kernel(pix, groups, rows_ref, ref_ref, scale_ref, energy_ref, gain_ref, planes_ref, evid_ref,
                 ext_ref, acc_ref, v_ref):
    chunks = pix // IMG

    def build(u, carry):
        off = pl.multiple_of(u * IMG, IMG)
        dst = pl.multiple_of(off + IMG, IMG)
        chunk = rows_ref[:, pl.ds(off, IMG)]
        wide = chunk.astype(jnp.float32)
        ext_ref[0, :, pl.ds(dst, IMG)] = pltpu.roll(wide, IMG - 1, 1).astype(jnp.bfloat16)
        ext_ref[1, :, pl.ds(dst, IMG)] = chunk
        ext_ref[2, :, pl.ds(dst, IMG)] = pltpu.roll(wide, 1, 1).astype(jnp.bfloat16)
        return carry

    lax.fori_loop(0, chunks, build, 0, unroll=32)
    ext_ref[:, :, 0:IMG] = ext_ref[:, :, pix:pix + IMG]
    ext_ref[:, :, pix + IMG:pix + 2 * IMG] = ext_ref[:, :, IMG:2 * IMG]

    acc_ref[...] = jnp.zeros_like(acc_ref)

    def products(j, carry):
        k0 = pl.multiple_of(j * TK, TK)
        tile = ref_ref[:, pl.ds(k0, TK)]
        for ai, a in enumerate(SHIFTS):
            start = pl.multiple_of(k0 + IMG * (1 - a), IMG)
            for bi in range(3):
                moved = ext_ref[bi, :, pl.ds(start, TK)]
                acc_ref[ai * 3 + bi] += lax.dot_general(
                    tile, moved, (((1,), (1,)), ((), ())), preferred_element_type=jnp.float32
                )
        return carry

    lax.fori_loop(0, pix // TK, products, 0)

    scale = scale_ref[...]
    half_energy = 0.5 * energy_ref[...]
    scores = [scale * (acc_ref[t] - half_energy) for t in range(9)]
    highest = jnp.max(scores[0], axis=0, keepdims=True)
    for t in range(1, 9):
        highest = jnp.maximum(highest, jnp.max(scores[t], axis=0, keepdims=True))
    total = jnp.sum(jnp.exp(scores[0] - highest), axis=0, keepdims=True)
    for t in range(1, 9):
        total = total + jnp.sum(jnp.exp(scores[t] - highest), axis=0, keepdims=True)
    evidence = highest + jnp.log(total)
    evid_ref[...] = evidence
    gain = gain_ref[...]
    gain_hi = gain.astype(jnp.bfloat16)
    gain_lo = (gain - gain_hi.astype(jnp.float32)).astype(jnp.bfloat16)
    depth = gain.shape[0]
    for t in range(9):
        weights = jnp.exp(scores[t] - evidence).astype(jnp.bfloat16)
        mixed = jnp.dot(gain_hi, weights, preferred_element_type=jnp.float32) + jnp.dot(
            gain_lo, weights, preferred_element_type=jnp.float32
        )
        mixed_hi = mixed.astype(jnp.bfloat16).astype(jnp.float32)
        v_ref[t, 0:depth] = mixed_hi
        v_ref[t, depth:2 * depth] = mixed - mixed_hi

    band = pix // groups
    width = band // IMG

    def plane_tiles(jj, carry):
        n0 = pl.multiple_of(jj * 2 * band, 2 * band)
        summed = jnp.zeros((2 * depth, 2 * band), jnp.float32)
        for ai, a in enumerate(SHIFTS):
            start = pl.multiple_of(n0 + IMG * (1 - a), IMG)
            for bi in range(3):
                summed = summed + jnp.dot(
                    v_ref[ai * 3 + bi].astype(jnp.bfloat16), ext_ref[bi, :, pl.ds(start, 2 * band)],
                    preferred_element_type=jnp.float32,
                )
        both = summed[0:depth] + summed[depth:2 * depth]
        for half in range(2):
            j = jj * 2 + half
            plane = both[:, half * band:(half + 1) * band]
            before = lax.rem(j + groups - 1, groups)
            for z in range(depth):
                for u in range(width):
                    row = z * (width + 1) + u
                    planes_ref[j, pl.ds(row, 1), :] = plane[z:z + 1, u * IMG:(u + 1) * IMG]
                row = z * (width + 1) + width
                planes_ref[before, pl.ds(row, 1), :] = plane[z:z + 1, 0:IMG]
        return carry

    lax.fori_loop(0, groups // 2, plane_tiles, 0)


def class_pass(rows_ext, templates, scale_row, energy_col, gain, pix, groups):
    rowcount = rows_ext.shape[0]
    refcount = templates.shape[0]
    depth = gain.shape[0]
    vmem = pl.BlockSpec(memory_space=pltpu.VMEM)
    flops = 2 * 9 * (refcount + 2 * depth) * rowcount * pix
    cost = pl.CostEstimate(
        flops=flops, transcendentals=10 * refcount * rowcount,
        bytes_accessed=rows_ext.size * 2 + templates.size * 2 + depth * pix * 4,
    )
    return pl.pallas_call(
        functools.partial(class_kernel, pix, groups),
        out_shape=(
            jax.ShapeDtypeStruct((groups, depth * (pix // groups // IMG + 1), IMG), jnp.float32),
            jax.ShapeDtypeStruct((1, rowcount), jnp.float32),
        ),
        in_specs=[vmem] * 5,
        out_specs=(vmem, vmem),
        scratch_shapes=[
            pltpu.VMEM((3, rowcount, pix + 2 * IMG), jnp.bfloat16),
            pltpu.VMEM((9, refcount, rowcount), jnp.float32),
            pltpu.VMEM((9, 2 * depth, rowcount), jnp.float32),
        ],
        compiler_params=pltpu.CompilerParams(vmem_limit_bytes=48 * 1024 * 1024),
        cost_estimate=cost,
    )(rows_ext, templates, scale_row, energy_col, gain)


def on_device(
    particles, particle_precision, particle_class, class_owner, references, insert_weights
):
    sources = lax.axis_size("dev")
    groups = lax.axis_size("grp")
    local_count, pix = particles.shape
    classes = class_owner.shape[0]
    owned_classes = references.shape[0]
    slot_depth = max(2, 2 * local_count // classes)
    labels = particle_class[:, 0]
    catalog = jnp.arange(classes, dtype=jnp.int32)
    position = jnp.sum(
        jnp.where(labels[:, None] == catalog[None, :], class_owner[None, :], 0), axis=1
    )
    ordinal = jnp.arange(local_count, dtype=jnp.int32)
    earlier = (labels[:, None] == labels[None, :]) & (ordinal[None, :] < ordinal[:, None])
    arrival = jnp.sum(earlier, axis=1)
    slot_index = position * slot_depth + arrival
    total_slots = classes * slot_depth
    extra = jnp.broadcast_to(particle_precision[:, None], (local_count, IMG))
    carried = jnp.concatenate([particles, extra], axis=1)
    width = pix + IMG
    outgoing = jnp.zeros((classes, slot_depth, width), carried.dtype)
    outgoing = outgoing.at[position, arrival].set(carried, unique_indices=True)
    arrived = lax.all_to_all(outgoing, "dev", split_axis=0, concat_axis=0, tiled=True)
    rows_ext = arrived.reshape(sources * slot_depth, width)
    scale_row = rows_ext[:, pix].astype(jnp.float32).reshape(1, sources * slot_depth)
    templates = references[0]
    energy_col = jnp.sum(jnp.square(templates.astype(jnp.float32)), axis=1).reshape(-1, 1)
    windows, class_evidence = class_pass(
        rows_ext, templates, scale_row, energy_col, insert_weights, pix, groups
    )
    stacked = class_evidence.reshape(sources, slot_depth)
    returned = lax.all_to_all(stacked, "dev", split_axis=0, concat_axis=0, tiled=True).reshape(
        total_slots
    )
    particle_evidence = jnp.take(returned, slot_index)
    depth = insert_weights.shape[0]
    band = IMG // groups
    here = lax.axis_index("grp")
    mine = lax.dynamic_index_in_dim(windows, here, 0, keepdims=False)
    for step in range(1, groups):
        part = lax.dynamic_index_in_dim(windows, lax.rem(here + step, groups), 0, keepdims=False)
        pairs = [(g, (g + step) % groups) for g in range(groups)]
        mine = mine + lax.ppermute(part, "grp", pairs)
    interp = upsample_table(VOL, IMG)
    across = jnp.dot(mine, interp.T, precision=lax.Precision.HIGH)
    rows_table = local_table(2 * band, band + 1)
    eye = jnp.eye(depth, dtype=jnp.float32)
    block = (rows_table[:, None, None, :] * eye[None, :, :, None]).reshape(
        2 * band * depth, depth * (band + 1)
    )
    volume = jnp.dot(block, across, precision=lax.Precision.HIGH).reshape(2 * band, depth, VOL)
    return (volume, particle_evidence)


def solution(mesh):
    placed = (
        P(("grp", "dev"), None),
        P(("grp", "dev")),
        P(("grp", "dev"), None),
        P(),
        P("dev", None, None),
        P("dev", None),
    )
    return jax.shard_map(
        on_device,
        mesh=mesh,
        in_specs=placed,
        out_specs=(P("grp", "dev", None), P(("grp", "dev"))),
        check_vma=False,
    )
```

```python
import functools

import jax
import jax.numpy as jnp
from jax import lax
from jax.experimental import pallas as pl
from jax.experimental.pallas import tpu as pltpu
from jax.sharding import PartitionSpec as P

IMG = 128
VOL = 256
SHIFTS = (-1, 0, 1)
TK = 16384
TN = 1024


def upsample_table(length, source):
    target = jnp.arange(length, dtype=jnp.int32)[:, None]
    anchor = jnp.arange(source, dtype=jnp.int32)[None, :]
    halves = target // 2
    lower = anchor == halves
    upper = anchor == (halves + 1) % source
    is_even = target % 2 == 0
    even_part = jnp.where(lower, 1.0, 0.0)
    odd_part = jnp.where(lower, 0.5, 0.0) + jnp.where(upper, 0.5, 0.0)
    return jnp.where(is_even, even_part, odd_part).astype(jnp.float32)


def local_table(rows, anchors):
    target = jnp.arange(rows, dtype=jnp.int32)[:, None]
    anchor = jnp.arange(anchors, dtype=jnp.int32)[None, :]
    halves = target // 2
    lower = anchor == halves
    upper = anchor == halves + 1
    is_even = target % 2 == 0
    even_part = jnp.where(lower, 1.0, 0.0)
    odd_part = jnp.where(lower, 0.5, 0.0) + jnp.where(upper, 0.5, 0.0)
    return jnp.where(is_even, even_part, odd_part).astype(jnp.float32)


def class_kernel(pix, groups, rows_ref, ref_ref, scale_ref, energy_ref, gain_ref, planes_ref, evid_ref,
                 ext_ref, acc_ref, v_ref):
    chunks = pix // IMG

    def build(u, carry):
        off = pl.multiple_of(u * IMG, IMG)
        dst = pl.multiple_of(off + IMG, IMG)
        chunk = rows_ref[:, pl.ds(off, IMG)]
        wide = chunk.astype(jnp.float32)
        ext_ref[0, :, pl.ds(dst, IMG)] = pltpu.roll(wide, IMG - 1, 1).astype(jnp.bfloat16)
        ext_ref[1, :, pl.ds(dst, IMG)] = chunk
        ext_ref[2, :, pl.ds(dst, IMG)] = pltpu.roll(wide, 1, 1).astype(jnp.bfloat16)
        return carry

    lax.fori_loop(0, chunks, build, 0, unroll=32)
    ext_ref[:, :, 0:IMG] = ext_ref[:, :, pix:pix + IMG]
    ext_ref[:, :, pix + IMG:pix + 2 * IMG] = ext_ref[:, :, IMG:2 * IMG]

    acc_ref[...] = jnp.zeros_like(acc_ref)

    def products(j, carry):
        k0 = pl.multiple_of(j * TK, TK)
        tile = ref_ref[:, pl.ds(k0, TK)]
        for ai, a in enumerate(SHIFTS):
            start = pl.multiple_of(k0 + IMG * (1 - a), IMG)
            for bi in range(3):
                moved = ext_ref[bi, :, pl.ds(start, TK)]
                acc_ref[ai * 3 + bi] += lax.dot_general(
                    tile, moved, (((1,), (1,)), ((), ())), preferred_element_type=jnp.float32
                )
        return carry

    lax.fori_loop(0, pix // TK, products, 0)

    scale = scale_ref[...]
    half_energy = 0.5 * energy_ref[...]
    scores = [scale * (acc_ref[t] - half_energy) for t in range(9)]
    highest = jnp.max(scores[0], axis=0, keepdims=True)
    for t in range(1, 9):
        highest = jnp.maximum(highest, jnp.max(scores[t], axis=0, keepdims=True))
    total = jnp.sum(jnp.exp(scores[0] - highest), axis=0, keepdims=True)
    for t in range(1, 9):
        total = total + jnp.sum(jnp.exp(scores[t] - highest), axis=0, keepdims=True)
    evidence = highest + jnp.log(total)
    evid_ref[...] = evidence
    gain = gain_ref[...]
    gain_hi = gain.astype(jnp.bfloat16)
    gain_lo = (gain - gain_hi.astype(jnp.float32)).astype(jnp.bfloat16)
    depth = gain.shape[0]
    for t in range(9):
        weights = jnp.exp(scores[t] - evidence).astype(jnp.bfloat16)
        mixed = jnp.dot(gain_hi, weights, preferred_element_type=jnp.float32) + jnp.dot(
            gain_lo, weights, preferred_element_type=jnp.float32
        )
        mixed_hi = mixed.astype(jnp.bfloat16).astype(jnp.float32)
        v_ref[t, 0:depth] = mixed_hi
        v_ref[t, depth:2 * depth] = mixed - mixed_hi

    band = pix // groups
    width = band // IMG

    def plane_tiles(jj, carry):
        n0 = pl.multiple_of(jj * 2 * band, 2 * band)
        summed = jnp.zeros((2 * depth, 2 * band), jnp.float32)
        for ai, a in enumerate(SHIFTS):
            start = pl.multiple_of(n0 + IMG * (1 - a), IMG)
            for bi in range(3):
                summed = summed + jnp.dot(
                    v_ref[ai * 3 + bi].astype(jnp.bfloat16), ext_ref[bi, :, pl.ds(start, 2 * band)],
                    preferred_element_type=jnp.float32,
                )
        both = summed[0:depth] + summed[depth:2 * depth]
        for half in range(2):
            j = jj * 2 + half
            plane = both[:, half * band:(half + 1) * band]
            before = lax.rem(j + groups - 1, groups)
            for z in range(depth):
                for u in range(width):
                    row = z * (width + 1) + u
                    planes_ref[j, pl.ds(row, 1), :] = plane[z:z + 1, u * IMG:(u + 1) * IMG]
                row = z * (width + 1) + width
                planes_ref[before, pl.ds(row, 1), :] = plane[z:z + 1, 0:IMG]
        return carry

    lax.fori_loop(0, groups // 2, plane_tiles, 0)


def class_pass(rows_ext, templates, scale_row, energy_col, gain, pix, groups):
    rowcount = rows_ext.shape[0]
    refcount = templates.shape[0]
    depth = gain.shape[0]
    vmem = pl.BlockSpec(memory_space=pltpu.VMEM)
    flops = 2 * 9 * (refcount + 2 * depth) * rowcount * pix
    cost = pl.CostEstimate(
        flops=flops, transcendentals=10 * refcount * rowcount,
        bytes_accessed=rows_ext.size * 2 + templates.size * 2 + depth * pix * 4,
    )
    return pl.pallas_call(
        functools.partial(class_kernel, pix, groups),
        out_shape=(
            jax.ShapeDtypeStruct((groups, depth * (pix // groups // IMG + 1), IMG), jnp.float32),
            jax.ShapeDtypeStruct((1, rowcount), jnp.float32),
        ),
        in_specs=[vmem] * 5,
        out_specs=(vmem, vmem),
        scratch_shapes=[
            pltpu.VMEM((3, rowcount, pix + 2 * IMG), jnp.bfloat16),
            pltpu.VMEM((9, refcount, rowcount), jnp.float32),
            pltpu.VMEM((9, 2 * depth, rowcount), jnp.float32),
        ],
        compiler_params=pltpu.CompilerParams(vmem_limit_bytes=48 * 1024 * 1024),
        cost_estimate=cost,
    )(rows_ext, templates, scale_row, energy_col, gain)


def on_device(
    particles, particle_precision, particle_class, class_owner, references, insert_weights
):
    sources = lax.axis_size("dev")
    groups = lax.axis_size("grp")
    local_count, pix = particles.shape
    classes = class_owner.shape[0]
    owned_classes = references.shape[0]
    slot_depth = max(2, 2 * local_count // classes)
    labels = particle_class[:, 0]
    catalog = jnp.arange(classes, dtype=jnp.int32)
    position = jnp.sum(
        jnp.where(labels[:, None] == catalog[None, :], class_owner[None, :], 0), axis=1
    )
    ordinal = jnp.arange(local_count, dtype=jnp.int32)
    earlier = (labels[:, None] == labels[None, :]) & (ordinal[None, :] < ordinal[:, None])
    arrival = jnp.sum(earlier, axis=1)
    slot_index = arrival * classes + position
    total_slots = classes * slot_depth
    placing = (jnp.arange(total_slots, dtype=jnp.int32)[:, None] == slot_index[None, :]).astype(
        jnp.bfloat16
    )
    extra = jnp.broadcast_to(particle_precision[:, None], (local_count, IMG))
    carried = jnp.concatenate([particles, extra], axis=1)
    width = pix + IMG
    outgoing = jnp.dot(placing, carried, preferred_element_type=jnp.float32).astype(jnp.bfloat16)
    outgoing = outgoing.reshape(slot_depth, sources, owned_classes * width)
    arrived = lax.all_to_all(outgoing, "dev", split_axis=1, concat_axis=1, tiled=True)
    rows_ext = arrived.reshape(slot_depth * sources, width)
    scale_row = rows_ext[:, pix].astype(jnp.float32).reshape(1, slot_depth * sources)
    templates = references[0]
    energy_col = jnp.sum(jnp.square(templates.astype(jnp.float32)), axis=1).reshape(-1, 1)
    windows, class_evidence = class_pass(
        rows_ext, templates, scale_row, energy_col, insert_weights, pix, groups
    )
    stacked = class_evidence.reshape(slot_depth, sources)
    returned = lax.all_to_all(stacked, "dev", split_axis=1, concat_axis=1, tiled=True).reshape(
        total_slots
    )
    windows, returned = lax.optimization_barrier((windows, returned))
    particle_evidence = jnp.take(returned, slot_index)
    depth = insert_weights.shape[0]
    band = IMG // groups
    here = lax.axis_index("grp")
    mine = lax.dynamic_index_in_dim(windows, here, 0, keepdims=False)
    for step in range(1, groups):
        part = lax.dynamic_index_in_dim(windows, lax.rem(here + step, groups), 0, keepdims=False)
        pairs = [(g, (g + step) % groups) for g in range(groups)]
        mine = mine + lax.ppermute(part, "grp", pairs)
    interp = upsample_table(VOL, IMG)
    across = jnp.dot(mine, interp.T, precision=lax.Precision.HIGH)
    rows_table = local_table(2 * band, band + 1)
    eye = jnp.eye(depth, dtype=jnp.float32)
    block = (rows_table[:, None, None, :] * eye[None, :, :, None]).reshape(
        2 * band * depth, depth * (band + 1)
    )
    volume = jnp.dot(block, across, precision=lax.Precision.HIGH).reshape(2 * band, depth, VOL)
    return (volume, particle_evidence)


def solution(mesh):
    placed = (
        P(("grp", "dev"), None),
        P(("grp", "dev")),
        P(("grp", "dev"), None),
        P(),
        P("dev", None, None),
        P("dev", None),
    )
    return jax.shard_map(
        on_device,
        mesh=mesh,
        in_specs=placed,
        out_specs=(P("grp", "dev", None), P(("grp", "dev"))),
        check_vma=False,
    )
```

```python
import functools

import jax
import jax.numpy as jnp
from jax import lax
from jax.experimental import pallas as pl
from jax.experimental.pallas import tpu as pltpu
from jax.sharding import PartitionSpec as P

IMG = 128
VOL = 256
SHIFTS = (-1, 0, 1)
TK = 16384
TN = 1024


def upsample_table(length, source):
    target = jnp.arange(length, dtype=jnp.int32)[:, None]
    anchor = jnp.arange(source, dtype=jnp.int32)[None, :]
    halves = target // 2
    lower = anchor == halves
    upper = anchor == (halves + 1) % source
    is_even = target % 2 == 0
    even_part = jnp.where(lower, 1.0, 0.0)
    odd_part = jnp.where(lower, 0.5, 0.0) + jnp.where(upper, 0.5, 0.0)
    return jnp.where(is_even, even_part, odd_part).astype(jnp.float32)


def local_table(rows, anchors):
    target = jnp.arange(rows, dtype=jnp.int32)[:, None]
    anchor = jnp.arange(anchors, dtype=jnp.int32)[None, :]
    halves = target // 2
    lower = anchor == halves
    upper = anchor == halves + 1
    is_even = target % 2 == 0
    even_part = jnp.where(lower, 1.0, 0.0)
    odd_part = jnp.where(lower, 0.5, 0.0) + jnp.where(upper, 0.5, 0.0)
    return jnp.where(is_even, even_part, odd_part).astype(jnp.float32)


def class_kernel(pix, groups, rows_ref, ref_ref, scale_ref, energy_ref, gain_ref, planes_ref, evid_ref,
                 ext_ref, acc_ref, v_ref):
    chunks = pix // IMG

    def build(u, carry):
        off = pl.multiple_of(u * IMG, IMG)
        dst = pl.multiple_of(off + IMG, IMG)
        chunk = rows_ref[:, pl.ds(off, IMG)]
        wide = chunk.astype(jnp.float32)
        ext_ref[0, :, pl.ds(dst, IMG)] = pltpu.roll(wide, IMG - 1, 1).astype(jnp.bfloat16)
        ext_ref[1, :, pl.ds(dst, IMG)] = chunk
        ext_ref[2, :, pl.ds(dst, IMG)] = pltpu.roll(wide, 1, 1).astype(jnp.bfloat16)
        return carry

    lax.fori_loop(0, chunks, build, 0, unroll=32)
    ext_ref[:, :, 0:IMG] = ext_ref[:, :, pix:pix + IMG]
    ext_ref[:, :, pix + IMG:pix + 2 * IMG] = ext_ref[:, :, IMG:2 * IMG]

    acc_ref[...] = jnp.zeros_like(acc_ref)

    def products(j, carry):
        k0 = pl.multiple_of(j * TK, TK)
        tile = ref_ref[:, pl.ds(k0, TK)]
        for ai, a in enumerate(SHIFTS):
            start = pl.multiple_of(k0 + IMG * (1 - a), IMG)
            for bi in range(3):
                moved = ext_ref[bi, :, pl.ds(start, TK)]
                acc_ref[ai * 3 + bi] += lax.dot_general(
                    tile, moved, (((1,), (1,)), ((), ())), preferred_element_type=jnp.float32
                )
        return carry

    lax.fori_loop(0, pix // TK, products, 0)

    scale = scale_ref[...]
    half_energy = 0.5 * energy_ref[...]
    scores = [scale * (acc_ref[t] - half_energy) for t in range(9)]
    highest = jnp.max(scores[0], axis=0, keepdims=True)
    for t in range(1, 9):
        highest = jnp.maximum(highest, jnp.max(scores[t], axis=0, keepdims=True))
    total = jnp.sum(jnp.exp(scores[0] - highest), axis=0, keepdims=True)
    for t in range(1, 9):
        total = total + jnp.sum(jnp.exp(scores[t] - highest), axis=0, keepdims=True)
    evidence = highest + jnp.log(total)
    evid_ref[...] = evidence
    gain = gain_ref[...]
    gain_hi = gain.astype(jnp.bfloat16)
    gain_lo = (gain - gain_hi.astype(jnp.float32)).astype(jnp.bfloat16)
    depth = gain.shape[0]
    for t in range(9):
        weights = jnp.exp(scores[t] - evidence).astype(jnp.bfloat16)
        mixed = jnp.dot(gain_hi, weights, preferred_element_type=jnp.float32) + jnp.dot(
            gain_lo, weights, preferred_element_type=jnp.float32
        )
        mixed_hi = mixed.astype(jnp.bfloat16).astype(jnp.float32)
        v_ref[t, 0:depth] = mixed_hi
        v_ref[t, depth:2 * depth] = mixed - mixed_hi

    band = pix // groups
    width = band // IMG

    def plane_tiles(jj, carry):
        n0 = pl.multiple_of(jj * 2 * band, 2 * band)
        summed = jnp.zeros((2 * depth, 2 * band), jnp.float32)
        for ai, a in enumerate(SHIFTS):
            start = pl.multiple_of(n0 + IMG * (1 - a), IMG)
            for bi in range(3):
                summed = summed + jnp.dot(
                    v_ref[ai * 3 + bi].astype(jnp.bfloat16), ext_ref[bi, :, pl.ds(start, 2 * band)],
                    preferred_element_type=jnp.float32,
                )
        both = summed[0:depth] + summed[depth:2 * depth]
        for half in range(2):
            j = jj * 2 + half
            plane = both[:, half * band:(half + 1) * band]
            before = lax.rem(j + groups - 1, groups)
            for z in range(depth):
                for u in range(width):
                    row = z * (width + 1) + u
                    planes_ref[j, pl.ds(row, 1), :] = plane[z:z + 1, u * IMG:(u + 1) * IMG]
                row = z * (width + 1) + width
                planes_ref[before, pl.ds(row, 1), :] = plane[z:z + 1, 0:IMG]
        return carry

    lax.fori_loop(0, groups // 2, plane_tiles, 0)


def class_pass(rows_ext, templates, scale_row, energy_col, gain, pix, groups):
    rowcount = rows_ext.shape[0]
    refcount = templates.shape[0]
    depth = gain.shape[0]
    vmem = pl.BlockSpec(memory_space=pltpu.VMEM)
    flops = 2 * 9 * (refcount + 2 * depth) * rowcount * pix
    cost = pl.CostEstimate(
        flops=flops, transcendentals=10 * refcount * rowcount,
        bytes_accessed=rows_ext.size * 2 + templates.size * 2 + depth * pix * 4,
    )
    return pl.pallas_call(
        functools.partial(class_kernel, pix, groups),
        out_shape=(
            jax.ShapeDtypeStruct((groups, depth * (pix // groups // IMG + 1), IMG), jnp.float32),
            jax.ShapeDtypeStruct((1, rowcount), jnp.float32),
        ),
        in_specs=[vmem] * 5,
        out_specs=(vmem, vmem),
        scratch_shapes=[
            pltpu.VMEM((3, rowcount, pix + 2 * IMG), jnp.bfloat16),
            pltpu.VMEM((9, refcount, rowcount), jnp.float32),
            pltpu.VMEM((9, 2 * depth, rowcount), jnp.float32),
        ],
        compiler_params=pltpu.CompilerParams(vmem_limit_bytes=48 * 1024 * 1024),
        cost_estimate=cost,
    )(rows_ext, templates, scale_row, energy_col, gain)


def on_device(
    particles, particle_precision, particle_class, class_owner, references, insert_weights
):
    sources = lax.axis_size("dev")
    groups = lax.axis_size("grp")
    local_count, pix = particles.shape
    classes = class_owner.shape[0]
    owned_classes = references.shape[0]
    slot_depth = max(2, 2 * local_count // classes)
    labels = particle_class[:, 0]
    catalog = jnp.arange(classes, dtype=jnp.int32)
    position = jnp.take(class_owner, labels, mode="clip")
    ordinal = jnp.arange(local_count, dtype=jnp.int32)
    earlier = (labels[:, None] == labels[None, :]) & (ordinal[None, :] < ordinal[:, None])
    arrival = jnp.sum(earlier, axis=1)
    slot_index = arrival * classes + position
    total_slots = classes * slot_depth
    placing = (jnp.arange(total_slots, dtype=jnp.int32)[:, None] == slot_index[None, :]).astype(
        jnp.bfloat16
    )
    extra = jnp.pad(particle_precision[:, None], ((0, 0), (0, IMG - 1)))
    carried = jnp.concatenate([particles, extra], axis=1)
    width = pix + IMG
    outgoing = jnp.dot(placing, carried, preferred_element_type=jnp.float32).astype(jnp.bfloat16)
    outgoing = outgoing.reshape(slot_depth, sources, owned_classes * width)
    arrived = lax.all_to_all(outgoing, "dev", split_axis=1, concat_axis=1, tiled=True)
    rows_ext = arrived.reshape(slot_depth * sources, width)
    scale_row = rows_ext[:, pix].astype(jnp.float32).reshape(1, slot_depth * sources)
    templates = references[0]
    energy_col = jnp.sum(jnp.square(templates.astype(jnp.float32)), axis=1).reshape(-1, 1)
    windows, class_evidence = class_pass(
        rows_ext, templates, scale_row, energy_col, insert_weights, pix, groups
    )
    stacked = class_evidence.reshape(slot_depth, sources)
    returned = lax.all_to_all(stacked, "dev", split_axis=1, concat_axis=1, tiled=True).reshape(
        total_slots
    )
    particle_evidence = jnp.take(returned, slot_index)
    depth = insert_weights.shape[0]
    band = IMG // groups
    here = lax.axis_index("grp")
    mine = lax.dynamic_index_in_dim(windows, here, 0, keepdims=False)
    for step in range(1, groups):
        part = lax.dynamic_index_in_dim(windows, lax.rem(here + step, groups), 0, keepdims=False)
        pairs = [(g, (g + step) % groups) for g in range(groups)]
        mine = mine + lax.ppermute(part, "grp", pairs)
    interp = upsample_table(VOL, IMG)
    across = jnp.dot(mine, interp.T, precision=lax.Precision.HIGH)
    rows_table = local_table(2 * band, band + 1)
    eye = jnp.eye(depth, dtype=jnp.float32)
    block = (rows_table[:, None, None, :] * eye[None, :, :, None]).reshape(
        2 * band * depth, depth * (band + 1)
    )
    volume = jnp.dot(block, across, precision=lax.Precision.HIGH).reshape(2 * band, depth, VOL)
    return (volume, particle_evidence)


def solution(mesh):
    placed = (
        P(("grp", "dev"), None),
        P(("grp", "dev")),
        P(("grp", "dev"), None),
        P(),
        P("dev", None, None),
        P("dev", None),
    )
    return jax.shard_map(
        on_device,
        mesh=mesh,
        in_specs=placed,
        out_specs=(P("grp", "dev", None), P(("grp", "dev"))),
        check_vma=False,
    )
```

```python
import functools

import jax
import jax.numpy as jnp
from jax import lax
from jax.experimental import pallas as pl
from jax.experimental.pallas import tpu as pltpu
from jax.sharding import PartitionSpec as P

IMG = 128
VOL = 256
SHIFTS = (-1, 0, 1)
TK = 16384
TN = 1024


def upsample_table(length, source):
    target = jnp.arange(length, dtype=jnp.int32)[:, None]
    anchor = jnp.arange(source, dtype=jnp.int32)[None, :]
    halves = target // 2
    lower = anchor == halves
    upper = anchor == (halves + 1) % source
    is_even = target % 2 == 0
    even_part = jnp.where(lower, 1.0, 0.0)
    odd_part = jnp.where(lower, 0.5, 0.0) + jnp.where(upper, 0.5, 0.0)
    return jnp.where(is_even, even_part, odd_part).astype(jnp.float32)


def local_table(rows, anchors):
    target = jnp.arange(rows, dtype=jnp.int32)[:, None]
    anchor = jnp.arange(anchors, dtype=jnp.int32)[None, :]
    halves = target // 2
    lower = anchor == halves
    upper = anchor == halves + 1
    is_even = target % 2 == 0
    even_part = jnp.where(lower, 1.0, 0.0)
    odd_part = jnp.where(lower, 0.5, 0.0) + jnp.where(upper, 0.5, 0.0)
    return jnp.where(is_even, even_part, odd_part).astype(jnp.float32)


def class_kernel(pix, groups, rows_ref, ref_ref, scale_ref, energy_ref, gain_ref, planes_ref, evid_ref,
                 ext_ref, acc_ref, v_ref):
    chunks = pix // IMG

    def build(u, carry):
        off = pl.multiple_of(u * IMG, IMG)
        dst = pl.multiple_of(off + IMG, IMG)
        chunk = rows_ref[:, pl.ds(off, IMG)]
        wide = chunk.astype(jnp.float32)
        ext_ref[0, :, pl.ds(dst, IMG)] = pltpu.roll(wide, IMG - 1, 1).astype(jnp.bfloat16)
        ext_ref[1, :, pl.ds(dst, IMG)] = chunk
        ext_ref[2, :, pl.ds(dst, IMG)] = pltpu.roll(wide, 1, 1).astype(jnp.bfloat16)
        return carry

    lax.fori_loop(0, chunks, build, 0, unroll=32)
    ext_ref[:, :, 0:IMG] = ext_ref[:, :, pix:pix + IMG]
    ext_ref[:, :, pix + IMG:pix + 2 * IMG] = ext_ref[:, :, IMG:2 * IMG]

    acc_ref[...] = jnp.zeros_like(acc_ref)

    def products(j, carry):
        k0 = pl.multiple_of(j * TK, TK)
        tile = ref_ref[:, pl.ds(k0, TK)]
        for ai, a in enumerate(SHIFTS):
            start = pl.multiple_of(k0 + IMG * (1 - a), IMG)
            for bi in range(3):
                moved = ext_ref[bi, :, pl.ds(start, TK)]
                acc_ref[ai * 3 + bi] += lax.dot_general(
                    tile, moved, (((1,), (1,)), ((), ())), preferred_element_type=jnp.float32
                )
        return carry

    lax.fori_loop(0, pix // TK, products, 0)

    scale = scale_ref[...]
    half_energy = 0.5 * energy_ref[...]
    scores = [scale * (acc_ref[t] - half_energy) for t in range(9)]
    highest = jnp.max(scores[0], axis=0, keepdims=True)
    for t in range(1, 9):
        highest = jnp.maximum(highest, jnp.max(scores[t], axis=0, keepdims=True))
    total = jnp.sum(jnp.exp(scores[0] - highest), axis=0, keepdims=True)
    for t in range(1, 9):
        total = total + jnp.sum(jnp.exp(scores[t] - highest), axis=0, keepdims=True)
    evidence = highest + jnp.log(total)
    evid_ref[...] = evidence
    gain = gain_ref[...]
    gain_hi = gain.astype(jnp.bfloat16)
    gain_lo = (gain - gain_hi.astype(jnp.float32)).astype(jnp.bfloat16)
    depth = gain.shape[0]
    for t in range(9):
        weights = jnp.exp(scores[t] - evidence).astype(jnp.bfloat16)
        mixed = jnp.dot(gain_hi, weights, preferred_element_type=jnp.float32) + jnp.dot(
            gain_lo, weights, preferred_element_type=jnp.float32
        )
        mixed_hi = mixed.astype(jnp.bfloat16).astype(jnp.float32)
        v_ref[t, 0:depth] = mixed_hi
        v_ref[t, depth:2 * depth] = mixed - mixed_hi

    band = pix // groups
    width = band // IMG

    def plane_tiles(jj, carry):
        n0 = pl.multiple_of(jj * 2 * band, 2 * band)
        summed = jnp.zeros((2 * depth, 2 * band), jnp.float32)
        for ai, a in enumerate(SHIFTS):
            start = pl.multiple_of(n0 + IMG * (1 - a), IMG)
            for bi in range(3):
                summed = summed + jnp.dot(
                    v_ref[ai * 3 + bi].astype(jnp.bfloat16), ext_ref[bi, :, pl.ds(start, 2 * band)],
                    preferred_element_type=jnp.float32,
                )
        both = summed[0:depth] + summed[depth:2 * depth]
        for half in range(2):
            j = jj * 2 + half
            plane = both[:, half * band:(half + 1) * band]
            before = lax.rem(j + groups - 1, groups)
            for z in range(depth):
                row = z * (width + 1)
                planes_ref[j, pl.ds(row, width), :] = plane[z:z + 1, :].reshape(width, IMG)
                row = z * (width + 1) + width
                planes_ref[before, pl.ds(row, 1), :] = plane[z:z + 1, 0:IMG]
        return carry

    lax.fori_loop(0, groups // 2, plane_tiles, 0)


def class_pass(rows_ext, templates, scale_row, energy_col, gain, pix, groups):
    rowcount = rows_ext.shape[0]
    refcount = templates.shape[0]
    depth = gain.shape[0]
    vmem = pl.BlockSpec(memory_space=pltpu.VMEM)
    flops = 2 * 9 * (refcount + 2 * depth) * rowcount * pix
    cost = pl.CostEstimate(
        flops=flops, transcendentals=10 * refcount * rowcount,
        bytes_accessed=rows_ext.size * 2 + templates.size * 2 + depth * pix * 4,
    )
    return pl.pallas_call(
        functools.partial(class_kernel, pix, groups),
        out_shape=(
            jax.ShapeDtypeStruct((groups, depth * (pix // groups // IMG + 1), IMG), jnp.float32),
            jax.ShapeDtypeStruct((1, rowcount), jnp.float32),
        ),
        in_specs=[vmem] * 5,
        out_specs=(vmem, vmem),
        scratch_shapes=[
            pltpu.VMEM((3, rowcount, pix + 2 * IMG), jnp.bfloat16),
            pltpu.VMEM((9, refcount, rowcount), jnp.float32),
            pltpu.VMEM((9, 2 * depth, rowcount), jnp.float32),
        ],
        compiler_params=pltpu.CompilerParams(vmem_limit_bytes=48 * 1024 * 1024),
        cost_estimate=cost,
    )(rows_ext, templates, scale_row, energy_col, gain)


def on_device(
    particles, particle_precision, particle_class, class_owner, references, insert_weights
):
    sources = lax.axis_size("dev")
    groups = lax.axis_size("grp")
    local_count, pix = particles.shape
    classes = class_owner.shape[0]
    owned_classes = references.shape[0]
    slot_depth = max(2, 2 * local_count // classes)
    labels = particle_class[:, 0]
    catalog = jnp.arange(classes, dtype=jnp.int32)
    position = jnp.sum(
        jnp.where(labels[:, None] == catalog[None, :], class_owner[None, :], 0), axis=1
    )
    ordinal = jnp.arange(local_count, dtype=jnp.int32)
    earlier = (labels[:, None] == labels[None, :]) & (ordinal[None, :] < ordinal[:, None])
    arrival = jnp.sum(earlier, axis=1)
    slot_index = arrival * classes + position
    total_slots = classes * slot_depth
    placing = (jnp.arange(total_slots, dtype=jnp.int32)[:, None] == slot_index[None, :]).astype(
        jnp.bfloat16
    )
    extra = jnp.broadcast_to(particle_precision[:, None], (local_count, IMG))
    carried = jnp.concatenate([particles, extra], axis=1)
    width = pix + IMG
    outgoing = jnp.dot(placing, carried, preferred_element_type=jnp.float32).astype(jnp.bfloat16)
    outgoing = outgoing.reshape(slot_depth, sources, owned_classes * width)
    arrived = lax.all_to_all(outgoing, "dev", split_axis=1, concat_axis=1, tiled=True)
    rows_ext = arrived.reshape(slot_depth * sources, width)
    scale_row = rows_ext[:, pix].astype(jnp.float32).reshape(1, slot_depth * sources)
    templates = references[0]
    energy_col = jnp.sum(jnp.square(templates.astype(jnp.float32)), axis=1).reshape(-1, 1)
    windows, class_evidence = class_pass(
        rows_ext, templates, scale_row, energy_col, insert_weights, pix, groups
    )
    stacked = class_evidence.reshape(slot_depth, sources)
    returned = lax.all_to_all(stacked, "dev", split_axis=1, concat_axis=1, tiled=True).reshape(
        total_slots
    )
    particle_evidence = jnp.take(returned, slot_index)
    depth = insert_weights.shape[0]
    band = IMG // groups
    here = lax.axis_index("grp")
    mine = lax.dynamic_index_in_dim(windows, here, 0, keepdims=False)
    for step in range(1, groups):
        part = lax.dynamic_index_in_dim(windows, lax.rem(here + step, groups), 0, keepdims=False)
        pairs = [(g, (g + step) % groups) for g in range(groups)]
        mine = mine + lax.ppermute(part, "grp", pairs)
    interp = upsample_table(VOL, IMG)
    across = jnp.dot(mine, interp.T, precision=lax.Precision.HIGH)
    rows_table = local_table(2 * band, band + 1)
    eye = jnp.eye(depth, dtype=jnp.float32)
    block = (rows_table[:, None, None, :] * eye[None, :, :, None]).reshape(
        2 * band * depth, depth * (band + 1)
    )
    volume = jnp.dot(block, across, precision=lax.Precision.HIGH).reshape(2 * band, depth, VOL)
    return (volume, particle_evidence)


def solution(mesh):
    placed = (
        P(("grp", "dev"), None),
        P(("grp", "dev")),
        P(("grp", "dev"), None),
        P(),
        P("dev", None, None),
        P("dev", None),
    )
    return jax.shard_map(
        on_device,
        mesh=mesh,
        in_specs=placed,
        out_specs=(P("grp", "dev", None), P(("grp", "dev"))),
        check_vma=False,
    )
```

```python
import functools

import jax
import jax.numpy as jnp
from jax import lax
from jax.experimental import pallas as pl
from jax.experimental.pallas import tpu as pltpu
from jax.sharding import PartitionSpec as P

IMG = 128
VOL = 256
SHIFTS = (-1, 0, 1)
TN = 1024


def upsample_table(length, source):
    target = jnp.arange(length, dtype=jnp.int32)[:, None]
    anchor = jnp.arange(source, dtype=jnp.int32)[None, :]
    halves = target // 2
    lower = anchor == halves
    upper = anchor == (halves + 1) % source
    is_even = target % 2 == 0
    even_part = jnp.where(lower, 1.0, 0.0)
    odd_part = jnp.where(lower, 0.5, 0.0) + jnp.where(upper, 0.5, 0.0)
    return jnp.where(is_even, even_part, odd_part).astype(jnp.float32)


def local_table(rows, anchors):
    target = jnp.arange(rows, dtype=jnp.int32)[:, None]
    anchor = jnp.arange(anchors, dtype=jnp.int32)[None, :]
    halves = target // 2
    lower = anchor == halves
    upper = anchor == halves + 1
    is_even = target % 2 == 0
    even_part = jnp.where(lower, 1.0, 0.0)
    odd_part = jnp.where(lower, 0.5, 0.0) + jnp.where(upper, 0.5, 0.0)
    return jnp.where(is_even, even_part, odd_part).astype(jnp.float32)


def class_kernel(pix, groups, rows_ref, ref_ref, scale_ref, energy_ref, gain_ref, planes_ref, evid_ref,
                 ext_ref, acc_ref, v_ref):
    chunks = pix // IMG

    def build(u, carry):
        off = pl.multiple_of(u * IMG, IMG)
        dst = pl.multiple_of(off + IMG, IMG)
        chunk = rows_ref[:, pl.ds(off, IMG)]
        wide = chunk.astype(jnp.float32)
        ext_ref[0, :, pl.ds(dst, IMG)] = pltpu.roll(wide, IMG - 1, 1).astype(jnp.bfloat16)
        ext_ref[1, :, pl.ds(dst, IMG)] = chunk
        ext_ref[2, :, pl.ds(dst, IMG)] = pltpu.roll(wide, 1, 1).astype(jnp.bfloat16)
        return carry

    lax.fori_loop(0, chunks, build, 0, unroll=32)
    ext_ref[:, :, 0:IMG] = ext_ref[:, :, pix:pix + IMG]
    ext_ref[:, :, pix + IMG:pix + 2 * IMG] = ext_ref[:, :, IMG:2 * IMG]

    tile = ref_ref[...]
    for ai, a in enumerate(SHIFTS):
        start = IMG * (1 - a)
        for bi in range(3):
            moved = ext_ref[bi, :, start:start + pix]
            acc_ref[ai * 3 + bi] = lax.dot_general(
                tile, moved, (((1,), (1,)), ((), ())), preferred_element_type=jnp.float32
            )

    scale = scale_ref[...]
    half_energy = 0.5 * energy_ref[...]
    scores = [scale * (acc_ref[t] - half_energy) for t in range(9)]
    highest = jnp.max(scores[0], axis=0, keepdims=True)
    for t in range(1, 9):
        highest = jnp.maximum(highest, jnp.max(scores[t], axis=0, keepdims=True))
    raised = [jnp.exp(scores[t] - highest) for t in range(9)]
    total = jnp.sum(raised[0], axis=0, keepdims=True)
    for t in range(1, 9):
        total = total + jnp.sum(raised[t], axis=0, keepdims=True)
    evidence = highest + jnp.log(total)
    inverse = 1.0 / total
    evid_ref[...] = evidence
    gain = gain_ref[...]
    gain_hi = gain.astype(jnp.bfloat16)
    gain_lo = (gain - gain_hi.astype(jnp.float32)).astype(jnp.bfloat16)
    depth = gain.shape[0]
    for t in range(9):
        weights = (raised[t] * inverse).astype(jnp.bfloat16)
        mixed = jnp.dot(gain_hi, weights, preferred_element_type=jnp.float32) + jnp.dot(
            gain_lo, weights, preferred_element_type=jnp.float32
        )
        mixed_hi = mixed.astype(jnp.bfloat16).astype(jnp.float32)
        v_ref[t, 0:depth] = mixed_hi
        v_ref[t, depth:2 * depth] = mixed - mixed_hi

    band = pix // groups
    width = band // IMG

    def plane_tiles(jj, carry):
        n0 = pl.multiple_of(jj * 2 * band, 2 * band)
        summed = jnp.zeros((2 * depth, 2 * band), jnp.float32)
        for ai, a in enumerate(SHIFTS):
            start = pl.multiple_of(n0 + IMG * (1 - a), IMG)
            for bi in range(3):
                summed = summed + jnp.dot(
                    v_ref[ai * 3 + bi].astype(jnp.bfloat16), ext_ref[bi, :, pl.ds(start, 2 * band)],
                    preferred_element_type=jnp.float32,
                )
        both = summed[0:depth] + summed[depth:2 * depth]
        for half in range(2):
            j = jj * 2 + half
            plane = both[:, half * band:(half + 1) * band]
            before = lax.rem(j + groups - 1, groups)
            for z in range(depth):
                for u in range(width):
                    row = z * (width + 1) + u
                    planes_ref[j, pl.ds(row, 1), :] = plane[z:z + 1, u * IMG:(u + 1) * IMG]
                row = z * (width + 1) + width
                planes_ref[before, pl.ds(row, 1), :] = plane[z:z + 1, 0:IMG]
        return carry

    lax.fori_loop(0, groups // 2, plane_tiles, 0)


def class_pass(rows_ext, templates, scale_row, energy_col, gain, pix, groups):
    rowcount = rows_ext.shape[0]
    refcount = templates.shape[0]
    depth = gain.shape[0]
    vmem = pl.BlockSpec(memory_space=pltpu.VMEM)
    flops = 2 * 9 * (refcount + 2 * depth) * rowcount * pix
    cost = pl.CostEstimate(
        flops=flops, transcendentals=10 * refcount * rowcount,
        bytes_accessed=rows_ext.size * 2 + templates.size * 2 + depth * pix * 4,
    )
    return pl.pallas_call(
        functools.partial(class_kernel, pix, groups),
        out_shape=(
            jax.ShapeDtypeStruct((groups, depth * (pix // groups // IMG + 1), IMG), jnp.float32),
            jax.ShapeDtypeStruct((1, rowcount), jnp.float32),
        ),
        in_specs=[vmem] * 5,
        out_specs=(vmem, vmem),
        scratch_shapes=[
            pltpu.VMEM((3, rowcount, pix + 2 * IMG), jnp.bfloat16),
            pltpu.VMEM((9, refcount, rowcount), jnp.float32),
            pltpu.VMEM((9, 2 * depth, rowcount), jnp.float32),
        ],
        compiler_params=pltpu.CompilerParams(vmem_limit_bytes=48 * 1024 * 1024),
        cost_estimate=cost,
    )(rows_ext, templates, scale_row, energy_col, gain)


def on_device(
    particles, particle_precision, particle_class, class_owner, references, insert_weights
):
    sources = lax.axis_size("dev")
    groups = lax.axis_size("grp")
    local_count, pix = particles.shape
    classes = class_owner.shape[0]
    owned_classes = references.shape[0]
    slot_depth = max(2, 2 * local_count // classes)
    labels = particle_class[:, 0]
    catalog = jnp.arange(classes, dtype=jnp.int32)
    position = jnp.sum(
        jnp.where(labels[:, None] == catalog[None, :], class_owner[None, :], 0), axis=1
    )
    ordinal = jnp.arange(local_count, dtype=jnp.int32)
    earlier = (labels[:, None] == labels[None, :]) & (ordinal[None, :] < ordinal[:, None])
    arrival = jnp.sum(earlier, axis=1)
    slot_index = arrival * classes + position
    total_slots = classes * slot_depth
    placing = (jnp.arange(total_slots, dtype=jnp.int32)[:, None] == slot_index[None, :]).astype(
        jnp.bfloat16
    )
    extra = jnp.broadcast_to(particle_precision[:, None], (local_count, IMG))
    carried = jnp.concatenate([particles, extra], axis=1)
    width = pix + IMG
    outgoing = jnp.dot(placing, carried, preferred_element_type=jnp.float32).astype(jnp.bfloat16)
    outgoing = outgoing.reshape(slot_depth, sources, owned_classes * width)
    arrived = lax.all_to_all(outgoing, "dev", split_axis=1, concat_axis=1, tiled=True)
    rows_ext = arrived.reshape(slot_depth * sources, width)
    scale_row = rows_ext[:, pix].astype(jnp.float32).reshape(1, slot_depth * sources)
    templates = references[0]
    energy_col = jnp.sum(jnp.square(templates.astype(jnp.float32)), axis=1).reshape(-1, 1)
    windows, class_evidence = class_pass(
        rows_ext, templates, scale_row, energy_col, insert_weights, pix, groups
    )
    stacked = class_evidence.reshape(slot_depth, sources)
    returned = lax.all_to_all(stacked, "dev", split_axis=1, concat_axis=1, tiled=True).reshape(
        total_slots
    )
    particle_evidence = jnp.take(returned, slot_index)
    depth = insert_weights.shape[0]
    band = IMG // groups
    here = lax.axis_index("grp")
    mine = lax.dynamic_index_in_dim(windows, here, 0, keepdims=False)
    for step in range(1, groups):
        part = lax.dynamic_index_in_dim(windows, lax.rem(here + step, groups), 0, keepdims=False)
        pairs = [(g, (g + step) % groups) for g in range(groups)]
        mine = mine + lax.ppermute(part, "grp", pairs)
    interp = upsample_table(VOL, IMG)
    across = jnp.dot(mine, interp.T, precision=lax.Precision.HIGH)
    rows_table = local_table(2 * band, band + 1)
    eye = jnp.eye(depth, dtype=jnp.float32)
    block = (rows_table[:, None, None, :] * eye[None, :, :, None]).reshape(
        2 * band * depth, depth * (band + 1)
    )
    volume = jnp.dot(block, across, precision=lax.Precision.HIGH).reshape(2 * band, depth, VOL)
    return (volume, particle_evidence)


def solution(mesh):
    placed = (
        P(("grp", "dev"), None),
        P(("grp", "dev")),
        P(("grp", "dev"), None),
        P(),
        P("dev", None, None),
        P("dev", None),
    )
    return jax.shard_map(
        on_device,
        mesh=mesh,
        in_specs=placed,
        out_specs=(P("grp", "dev", None), P(("grp", "dev"))),
        check_vma=False,
    )
```

```python
import functools

import jax
import jax.numpy as jnp
from jax import lax
from jax.experimental import pallas as pl
from jax.experimental.pallas import tpu as pltpu
from jax.sharding import PartitionSpec as P

IMG = 128
VOL = 256
SHIFTS = (-1, 0, 1)
TK = 16384
TN = 1024


def upsample_table(length, source):
    target = jnp.arange(length, dtype=jnp.int32)[:, None]
    anchor = jnp.arange(source, dtype=jnp.int32)[None, :]
    halves = target // 2
    lower = anchor == halves
    upper = anchor == (halves + 1) % source
    is_even = target % 2 == 0
    even_part = jnp.where(lower, 1.0, 0.0)
    odd_part = jnp.where(lower, 0.5, 0.0) + jnp.where(upper, 0.5, 0.0)
    return jnp.where(is_even, even_part, odd_part).astype(jnp.float32)


def local_table(rows, anchors):
    target = jnp.arange(rows, dtype=jnp.int32)[:, None]
    anchor = jnp.arange(anchors, dtype=jnp.int32)[None, :]
    halves = target // 2
    lower = anchor == halves
    upper = anchor == halves + 1
    is_even = target % 2 == 0
    even_part = jnp.where(lower, 1.0, 0.0)
    odd_part = jnp.where(lower, 0.5, 0.0) + jnp.where(upper, 0.5, 0.0)
    return jnp.where(is_even, even_part, odd_part).astype(jnp.float32)


def class_kernel(pix, groups, rows_ref, ref_ref, scale_ref, energy_ref, gain_ref, planes_ref, evid_ref,
                 ext_ref, acc_ref, v_ref):
    chunks = pix // IMG

    def build(u, carry):
        off = pl.multiple_of(u * IMG, IMG)
        dst = pl.multiple_of(off + IMG, IMG)
        chunk = rows_ref[:, pl.ds(off, IMG)]
        wide = chunk.astype(jnp.float32)
        ext_ref[0, :, pl.ds(dst, IMG)] = pltpu.roll(wide, IMG - 1, 1).astype(jnp.bfloat16)
        ext_ref[1, :, pl.ds(dst, IMG)] = chunk
        ext_ref[2, :, pl.ds(dst, IMG)] = pltpu.roll(wide, 1, 1).astype(jnp.bfloat16)
        return carry

    lax.fori_loop(0, chunks, build, 0, unroll=32)
    ext_ref[:, :, 0:IMG] = ext_ref[:, :, pix:pix + IMG]
    ext_ref[:, :, pix + IMG:pix + 2 * IMG] = ext_ref[:, :, IMG:2 * IMG]

    acc_ref[...] = jnp.zeros_like(acc_ref)

    def products(j, carry):
        k0 = pl.multiple_of(j * TK, TK)
        tile = ref_ref[:, pl.ds(k0, TK)]
        for ai, a in enumerate(SHIFTS):
            start = pl.multiple_of(k0 + IMG * (1 - a), IMG)
            for bi in range(3):
                moved = ext_ref[bi, :, pl.ds(start, TK)]
                acc_ref[ai * 3 + bi] += lax.dot_general(
                    tile, moved, (((1,), (1,)), ((), ())), preferred_element_type=jnp.float32
                )
        return carry

    lax.fori_loop(0, pix // TK, products, 0)

    scale = scale_ref[...]
    half_energy = 0.5 * energy_ref[...]
    scores = [scale * (acc_ref[t] - half_energy) for t in range(9)]
    highest = jnp.max(scores[0], axis=0, keepdims=True)
    for t in range(1, 9):
        highest = jnp.maximum(highest, jnp.max(scores[t], axis=0, keepdims=True))
    total = jnp.sum(jnp.exp(scores[0] - highest), axis=0, keepdims=True)
    for t in range(1, 9):
        total = total + jnp.sum(jnp.exp(scores[t] - highest), axis=0, keepdims=True)
    evidence = highest + jnp.log(total)
    evid_ref[...] = evidence
    gain = gain_ref[...]
    gain_hi = gain.astype(jnp.bfloat16)
    gain_lo = (gain - gain_hi.astype(jnp.float32)).astype(jnp.bfloat16)
    depth = gain.shape[0]
    stacked = jnp.concatenate([gain_hi, gain_lo], axis=0)
    for t in range(9):
        weights = jnp.exp(scores[t] - evidence).astype(jnp.bfloat16)
        pair = jnp.dot(stacked, weights, preferred_element_type=jnp.float32)
        mixed = pair[0:depth] + pair[depth:2 * depth]
        mixed_hi = mixed.astype(jnp.bfloat16).astype(jnp.float32)
        v_ref[t, 0:depth] = mixed_hi
        v_ref[t, depth:2 * depth] = mixed - mixed_hi

    band = pix // groups
    width = band // IMG

    def plane_tiles(jj, carry):
        n0 = pl.multiple_of(jj * 2 * band, 2 * band)
        summed = jnp.zeros((2 * depth, 2 * band), jnp.float32)
        for ai, a in enumerate(SHIFTS):
            start = pl.multiple_of(n0 + IMG * (1 - a), IMG)
            for bi in range(3):
                summed = summed + jnp.dot(
                    v_ref[ai * 3 + bi].astype(jnp.bfloat16), ext_ref[bi, :, pl.ds(start, 2 * band)],
                    preferred_element_type=jnp.float32,
                )
        both = summed[0:depth] + summed[depth:2 * depth]
        for half in range(2):
            j = jj * 2 + half
            plane = both[:, half * band:(half + 1) * band]
            before = lax.rem(j + groups - 1, groups)
            for z in range(depth):
                for u in range(width):
                    row = z * (width + 1) + u
                    planes_ref[j, pl.ds(row, 1), :] = plane[z:z + 1, u * IMG:(u + 1) * IMG]
                row = z * (width + 1) + width
                planes_ref[before, pl.ds(row, 1), :] = plane[z:z + 1, 0:IMG]
        return carry

    lax.fori_loop(0, groups // 2, plane_tiles, 0)


def class_pass(rows_ext, templates, scale_row, energy_col, gain, pix, groups):
    rowcount = rows_ext.shape[0]
    refcount = templates.shape[0]
    depth = gain.shape[0]
    vmem = pl.BlockSpec(memory_space=pltpu.VMEM)
    flops = 2 * 9 * (refcount + 2 * depth) * rowcount * pix
    cost = pl.CostEstimate(
        flops=flops, transcendentals=10 * refcount * rowcount,
        bytes_accessed=rows_ext.size * 2 + templates.size * 2 + depth * pix * 4,
    )
    return pl.pallas_call(
        functools.partial(class_kernel, pix, groups),
        out_shape=(
            jax.ShapeDtypeStruct((groups, depth * (pix // groups // IMG + 1), IMG), jnp.float32),
            jax.ShapeDtypeStruct((1, rowcount), jnp.float32),
        ),
        in_specs=[vmem] * 5,
        out_specs=(vmem, vmem),
        scratch_shapes=[
            pltpu.VMEM((3, rowcount, pix + 2 * IMG), jnp.bfloat16),
            pltpu.VMEM((9, refcount, rowcount), jnp.float32),
            pltpu.VMEM((9, 2 * depth, rowcount), jnp.float32),
        ],
        compiler_params=pltpu.CompilerParams(vmem_limit_bytes=48 * 1024 * 1024),
        cost_estimate=cost,
    )(rows_ext, templates, scale_row, energy_col, gain)


def on_device(
    particles, particle_precision, particle_class, class_owner, references, insert_weights
):
    sources = lax.axis_size("dev")
    groups = lax.axis_size("grp")
    local_count, pix = particles.shape
    classes = class_owner.shape[0]
    owned_classes = references.shape[0]
    slot_depth = max(2, 2 * local_count // classes)
    labels = particle_class[:, 0]
    catalog = jnp.arange(classes, dtype=jnp.int32)
    position = jnp.sum(
        jnp.where(labels[:, None] == catalog[None, :], class_owner[None, :], 0), axis=1
    )
    ordinal = jnp.arange(local_count, dtype=jnp.int32)
    earlier = (labels[:, None] == labels[None, :]) & (ordinal[None, :] < ordinal[:, None])
    arrival = jnp.sum(earlier, axis=1)
    slot_index = arrival * classes + position
    total_slots = classes * slot_depth
    placing = (jnp.arange(total_slots, dtype=jnp.int32)[:, None] == slot_index[None, :]).astype(
        jnp.bfloat16
    )
    extra = jnp.broadcast_to(particle_precision[:, None], (local_count, IMG))
    carried = jnp.concatenate([particles, extra], axis=1)
    width = pix + IMG
    outgoing = jnp.dot(placing, carried, preferred_element_type=jnp.float32).astype(jnp.bfloat16)
    outgoing = outgoing.reshape(slot_depth, sources, owned_classes * width)
    arrived = lax.all_to_all(outgoing, "dev", split_axis=1, concat_axis=1, tiled=True)
    rows_ext = arrived.reshape(slot_depth * sources, width)
    scale_row = rows_ext[:, pix].astype(jnp.float32).reshape(1, slot_depth * sources)
    templates = references[0]
    energy_col = jnp.sum(jnp.square(templates.astype(jnp.float32)), axis=1).reshape(-1, 1)
    windows, class_evidence = class_pass(
        rows_ext, templates, scale_row, energy_col, insert_weights, pix, groups
    )
    stacked = class_evidence.reshape(slot_depth, sources)
    returned = lax.all_to_all(stacked, "dev", split_axis=1, concat_axis=1, tiled=True).reshape(
        total_slots
    )
    particle_evidence = jnp.take(returned, slot_index)
    depth = insert_weights.shape[0]
    band = IMG // groups
    here = lax.axis_index("grp")
    mine = lax.dynamic_index_in_dim(windows, here, 0, keepdims=False)
    for step in range(1, groups):
        part = lax.dynamic_index_in_dim(windows, lax.rem(here + step, groups), 0, keepdims=False)
        pairs = [(g, (g + step) % groups) for g in range(groups)]
        mine = mine + lax.ppermute(part, "grp", pairs)
    interp = upsample_table(VOL, IMG)
    across = jnp.dot(mine, interp.T, precision=lax.Precision.HIGH)
    rows_table = local_table(2 * band, band + 1)
    eye = jnp.eye(depth, dtype=jnp.float32)
    block = (rows_table[:, None, None, :] * eye[None, :, :, None]).reshape(
        2 * band * depth, depth * (band + 1)
    )
    volume = jnp.dot(block, across, precision=lax.Precision.HIGH).reshape(2 * band, depth, VOL)
    return (volume, particle_evidence)


def solution(mesh):
    placed = (
        P(("grp", "dev"), None),
        P(("grp", "dev")),
        P(("grp", "dev"), None),
        P(),
        P("dev", None, None),
        P("dev", None),
    )
    return jax.shard_map(
        on_device,
        mesh=mesh,
        in_specs=placed,
        out_specs=(P("grp", "dev", None), P(("grp", "dev"))),
        check_vma=False,
    )
```
